128 devices in a mesh: blk: 32 (over x, z, y_hi), band: 4 (over y_lo, core).
Axes of the slice: x: 4, y: 4 (y_hi: 2, y_lo: 2; y = y_hi * 2 + y_lo), z: 4, core: 2. Of those that a mesh axis runs over, the one named last changes fastest.
Arguments:
- coarse_kernel: bfloat16 [64, 512, 512], P('blk'), may hold values from -6 to 6
- interp_index: int32 [256, 8, 4], P('blk'), may hold values from 0 to 63, as said below
- interp_weight: float32 [256, 8, 4], P('blk'), may hold values from 0.1 to 1
- stop_order: int32 [8], replicated, may hold values from 0 to 7, each once
- intersection: bfloat16 [256, 512, 512], P('blk'), may hold values from -0.25 to 0.25
- trial_vectors: bfloat16 [256, 512, 128], P('blk', 'band'), may hold values from -0.09375 to 0.09375
Outputs:
- hamiltonian: bfloat16 [256, 8, 512, 512], P('blk', None, None, 'band')
- kernel_product: bfloat16 [256, 512, 128], P('blk', 'band')
The draws below stay inside these ranges and needn't reach their ends.
Inputs may be any that keep to these rules, and one draw needn't show every extreme that they name: `interp_index`: A fine k-point k lies on blk index i = k // 8; blk index j holds the coarse k-points j * 2 to (j + 1) * 2 - 1. The four coarse k-points named for k (j = 0, 1, 2, 3) lie on blk indices i - 1, i, i, i + 1, taken modulo the number of blk indices. `stop_order`: each of 0 to 7 once.
All inputs are finite; a program needn't handle non-finite values.
Results may differ from the reference program's by a relative error of at most 0.015.
Values may be sent and summed in bfloat16 or wider, within the bound.
No kernel may reach another device: no remote copies, remote signals or barrier semaphores. Data moves between devices by JAX's collectives and lax.ppermute only.
A program may use at most 128 MiB of HBM per device.

```python
import jax
import jax.numpy as jnp
from jax import lax

B = 512
V = 128
STOPS = 8
F_DEV = 8
NC_DEV = 2
NF = 256
NC = 64


def draw_interp_index(key, part):
    fine_points = jnp.arange(NF, dtype=jnp.int32)
    holder = fine_points // F_DEV
    cycle_length = NF // F_DEV
    corner_shift = jnp.array([-1, 0, 0, 1], dtype=jnp.int32)
    owners = jnp.mod(holder[:, None, None] + corner_shift[None, None, :], cycle_length)
    local_pick = jax.random.randint(key, (NF, STOPS, 4), 0, NC_DEV, dtype=jnp.int32)
    local_pick = local_pick.at[0, 0, 1].set(0)
    local_pick = local_pick.at[NF - 1, 0, 1].set(NC_DEV - 1)
    return (owners * NC_DEV + local_pick).astype(jnp.int32)


def levels(own_key, dims, shards, least, high):
    def one(position, shards_of):
        steps = jax.random.uniform(jax.random.fold_in(jax.random.fold_in(own_key, 6), position), (shards_of,), jnp.float32, least / len(shards), high / len(shards))
        return jnp.repeat(jnp.exp(steps), dims[position] // shards_of).reshape((-1,) + (1,) * (len(dims) - position - 1))

    loudness = one(*shards[0])
    for cut in shards[1:]:
        loudness = loudness * one(*cut)
    return loudness


def normal_values(own_key, shape, spread, reach, split=(), kind=jnp.bfloat16):
    values = spread * jax.random.normal(own_key, shape, jnp.float32)
    if split:
        values = values * levels(own_key, shape, split, -0.22, 0.18)
    return jnp.clip(values, -reach, reach).astype(kind)


def setup_inputs(seed: int = 0) -> dict:
    key_list = jax.random.split(jax.random.key(seed), 7)
    return {
        "coarse_kernel": normal_values(key_list[0], (NC, B, B), 1.0, 6.0, ((0, 32),)),
        "interp_index": draw_interp_index(jax.random.fold_in(key_list[6], 71), 0),
        "interp_weight": jnp.clip(0.1 + 0.9 * jax.random.uniform(key_list[2], (NF, STOPS, 4), jnp.float32) ** levels(key_list[2], (NF, STOPS, 4), ((0, 32),), -0.2, 0.2), 0.1, 1.0),
        "stop_order": jax.random.permutation(key_list[3], STOPS).astype(jnp.int32),
        "intersection": normal_values(key_list[4], (NF, B, B), B ** -0.5, 0.25, ((0, 32),)),
        "trial_vectors": normal_values(key_list[5], (NF, B, V), (1.0 / (STOPS * B) ** 0.5), 0.09375, ((0, 32), (1, 4))),
    }


def reference(coarse_kernel, interp_index, interp_weight, stop_order, intersection, trial_vectors):
    order_index = jnp.take(interp_index, stop_order, axis=1)
    order_weight = jnp.take(interp_weight, stop_order, axis=1)
    shifts = (jnp.arange(STOPS, dtype=jnp.int32) + 1) * F_DEV

    def one_point(packed):
        fine_point, index_point, weight_point, intersection_point = packed
        intersection_wide = intersection_point.astype(jnp.float32)

        def one_stop(stop_pack):
            index_stop, weight_stop = stop_pack
            blocks = jnp.take(coarse_kernel, index_stop, axis=0).astype(jnp.float32)
            kernel = jnp.sum(weight_stop[:, None, None] * blocks, axis=0).astype(jnp.bfloat16)
            rotated = jnp.dot(kernel.astype(jnp.float32), intersection_wide, precision=lax.Precision.HIGHEST).astype(jnp.bfloat16)
            return jnp.dot(intersection_wide.T, rotated.astype(jnp.float32), precision=lax.Precision.HIGHEST).astype(jnp.bfloat16)

        blocks_out = lax.map(one_stop, (index_point, weight_point))
        source_ids = jnp.mod(fine_point - shifts, NF).astype(jnp.int32)
        sources = jnp.take(trial_vectors, source_ids, axis=0).astype(jnp.float32)
        product = jnp.einsum('sac,scv->av', blocks_out.astype(jnp.float32), sources, precision=lax.Precision.HIGHEST)
        return blocks_out, product.astype(jnp.bfloat16)

    fine_points = jnp.arange(NF, dtype=jnp.int32)
    hamiltonian, kernel_product = lax.map(one_point, (fine_points, order_index, order_weight, intersection))
    return hamiltonian, kernel_product
```

```python
import functools

import jax
import jax.numpy as jnp
from jax import lax
from jax.experimental import pallas as pl
from jax.experimental.pallas import tpu as pltpu
from jax.sharding import PartitionSpec as P


def shifted(value, axis, steps):
    count = lax.axis_size(axis)
    pairs = [(source, (source + steps) % count) for source in range(count)]
    return lax.ppermute(value, axis, pairs)


def sandwich_kernel(slot_ref, band_ref, weight_ref, before_ref, local_ref, after_ref,
                    inter_ref, right_ref, trial_ref, ham_ref, part_ref, prod_ref, acc_ref,
                    *, blocks_dev, stop_count, corner_count):
    k = pl.program_id(0)
    s = pl.program_id(1)

    @pl.when(s == 0)
    def _():
        right = right_ref[0]
        for slot in range(blocks_dev):
            for group, source in enumerate((before_ref, local_ref, after_ref)):
                prod_ref[group * blocks_dev + slot] = jnp.dot(
                    source[slot], right, preferred_element_type=jnp.float32)
        acc_ref[...] = jnp.zeros_like(acc_ref)

    base = (k * stop_count + s) * corner_count
    rotated = weight_ref[base] * prod_ref[slot_ref[base]]
    for j in range(1, corner_count):
        rotated = rotated + weight_ref[base + j] * prod_ref[slot_ref[base + j]]
    rotated = rotated.astype(jnp.bfloat16)
    ham = lax.dot_general(
        inter_ref[0], rotated, (((0,), (0,)), ((), ())), preferred_element_type=jnp.float32
    ).astype(jnp.bfloat16)
    ham_ref[0, 0] = ham
    acc_ref[...] += jnp.dot(ham, trial_ref[0, 0], preferred_element_type=jnp.float32)

    @pl.when(s == stop_count - 1)
    def _():
        part_ref[0] = acc_ref[...].astype(jnp.bfloat16)


def on_device(coarse_kernel, interp_index, interp_weight, stop_order, intersection, trial_vectors):
    blocks_dev = coarse_kernel.shape[0]
    fine_dev = intersection.shape[0]
    column_count = trial_vectors.shape[1]
    vector_count = trial_vectors.shape[2]
    block_order = intersection.shape[1]
    stop_count = stop_order.shape[0]
    corner_count = interp_index.shape[2]
    cycle_length = lax.axis_size("blk")
    total_coarse = blocks_dev * cycle_length
    position = lax.axis_index("blk")
    band = lax.axis_index("band")

    before = shifted(coarse_kernel, "blk", 1)
    after = shifted(coarse_kernel, "blk", -1)
    sources = jnp.stack(
        [shifted(trial_vectors, "blk", station + 1) for station in range(stop_count)])

    order_index = jnp.take(interp_index, stop_order, axis=1)
    order_weight = jnp.take(interp_weight, stop_order, axis=1)
    window_slots = 3 * blocks_dev
    local_index = jnp.mod(order_index - (position - 1) * blocks_dev, total_coarse)
    slot_group = local_index // blocks_dev
    slot_index = jnp.clip(slot_group, 0, 2) * blocks_dev + jnp.mod(local_index, blocks_dev)
    slot_index = jnp.clip(slot_index, 0, window_slots - 1).astype(jnp.int32).reshape(-1)
    weights = order_weight.astype(jnp.float32).reshape(-1)
    band_index = jnp.reshape(band, (1,)).astype(jnp.int32)

    kernel = functools.partial(
        sandwich_kernel, blocks_dev=blocks_dev, stop_count=stop_count, corner_count=corner_count)
    whole = pl.BlockSpec((blocks_dev, block_order, block_order), lambda k, s, sl, bd: (0, 0, 0))
    grid_spec = pltpu.PrefetchScalarGridSpec(
        num_scalar_prefetch=2,
        grid=(fine_dev, stop_count),
        in_specs=[
            pl.BlockSpec(memory_space=pltpu.SMEM),
            whole,
            whole,
            whole,
            pl.BlockSpec((1, block_order, block_order), lambda k, s, sl, bd: (k, 0, 0)),
            pl.BlockSpec((1, block_order, column_count), lambda k, s, sl, bd: (k, 0, bd[0])),
            pl.BlockSpec((1, 1, column_count, vector_count), lambda k, s, sl, bd: (s, k, 0, 0)),
        ],
        out_specs=[
            pl.BlockSpec((1, 1, block_order, column_count), lambda k, s, sl, bd: (k, s, 0, 0)),
            pl.BlockSpec((1, block_order, vector_count), lambda k, s, sl, bd: (k, 0, 0)),
        ],
        scratch_shapes=[
            pltpu.VMEM((window_slots, block_order, column_count), jnp.float32),
            pltpu.VMEM((block_order, vector_count), jnp.float32),
        ],
    )
    hamiltonian, partial_value = pl.pallas_call(
        kernel,
        grid_spec=grid_spec,
        out_shape=[
            jax.ShapeDtypeStruct((fine_dev, stop_count, block_order, column_count), jnp.bfloat16),
            jax.ShapeDtypeStruct((fine_dev, block_order, vector_count), jnp.bfloat16),
        ],
        compiler_params=pltpu.CompilerParams(
            dimension_semantics=("arbitrary", "arbitrary"), vmem_limit_bytes=48 * 1024 * 1024),
    )(slot_index, band_index, weights, before, coarse_kernel, after, intersection, intersection,
      sources)
    product_share = lax.psum_scatter(partial_value, "band", scatter_dimension=1, tiled=True)
    return (hamiltonian, product_share)


def solution(mesh):
    placed = (
        P("blk", None, None),
        P("blk", None, None),
        P("blk", None, None),
        P(),
        P("blk", None, None),
        P("blk", "band", None),
    )
    return jax.shard_map(
        on_device,
        mesh=mesh,
        in_specs=placed,
        out_specs=(P("blk", None, None, "band"), P("blk", "band", None)),
        check_vma=False,
    )
```

```python
import functools

import jax
import jax.numpy as jnp
from jax import lax
from jax.experimental import pallas as pl
from jax.experimental.pallas import tpu as pltpu
from jax.sharding import PartitionSpec as P


def shifted(value, axis, steps):
    count = lax.axis_size(axis)
    pairs = [(source, (source + steps) % count) for source in range(count)]
    return lax.ppermute(value, axis, pairs)


def sandwich_kernel(slot_ref, band_ref, weight_ref, before_ref, local_ref, after_ref,
                    inter_ref, right_ref, ham_ref, prod_ref, left_ref,
                    *, blocks_dev, stop_count, corner_count):
    k = pl.program_id(0)
    s = pl.program_id(1)

    @pl.when(s == 0)
    def _():
        right = right_ref[0]
        for slot in range(blocks_dev):
            for group, source in enumerate((before_ref, local_ref, after_ref)):
                prod_ref[group * blocks_dev + slot] = jnp.dot(
                    source[slot], right, preferred_element_type=jnp.float32)
        left_ref[...] = inter_ref[0].T

    base = (k * stop_count + s) * corner_count
    rotated = weight_ref[base] * prod_ref[slot_ref[base]]
    for j in range(1, corner_count):
        rotated = rotated + weight_ref[base + j] * prod_ref[slot_ref[base + j]]
    rotated = rotated.astype(jnp.bfloat16)
    ham_ref[0, 0] = jnp.dot(
        left_ref[...], rotated, preferred_element_type=jnp.float32).astype(jnp.bfloat16)


def product_kernel(ham_ref, trial_ref, part_ref, *, stop_count):
    acc = jnp.dot(ham_ref[0, 0], trial_ref[0, 0], preferred_element_type=jnp.float32)
    for s in range(1, stop_count):
        acc = acc + jnp.dot(ham_ref[0, s], trial_ref[s, 0], preferred_element_type=jnp.float32)
    part_ref[0] = acc.astype(jnp.bfloat16)


def on_device(coarse_kernel, interp_index, interp_weight, stop_order, intersection, trial_vectors):
    blocks_dev = coarse_kernel.shape[0]
    fine_dev = intersection.shape[0]
    column_count = trial_vectors.shape[1]
    vector_count = trial_vectors.shape[2]
    block_order = intersection.shape[1]
    stop_count = stop_order.shape[0]
    corner_count = interp_index.shape[2]
    cycle_length = lax.axis_size("blk")
    total_coarse = blocks_dev * cycle_length
    position = lax.axis_index("blk")
    band = lax.axis_index("band")

    before = shifted(coarse_kernel, "blk", 1)
    after = shifted(coarse_kernel, "blk", -1)
    before, after, trial_vectors = lax.optimization_barrier((before, after, trial_vectors))
    sources = jnp.stack(
        [shifted(trial_vectors, "blk", station + 1) for station in range(stop_count)])

    order_index = jnp.take(interp_index, stop_order, axis=1)
    order_weight = jnp.take(interp_weight, stop_order, axis=1)
    window_slots = 3 * blocks_dev
    local_index = jnp.mod(order_index - (position - 1) * blocks_dev, total_coarse)
    slot_group = local_index // blocks_dev
    slot_index = jnp.clip(slot_group, 0, 2) * blocks_dev + jnp.mod(local_index, blocks_dev)
    slot_index = jnp.clip(slot_index, 0, window_slots - 1).astype(jnp.int32).reshape(-1)
    weights = order_weight.astype(jnp.float32).reshape(-1)
    band_index = jnp.reshape(band, (1,)).astype(jnp.int32)

    kernel = functools.partial(
        sandwich_kernel, blocks_dev=blocks_dev, stop_count=stop_count, corner_count=corner_count)
    whole = pl.BlockSpec((blocks_dev, block_order, block_order), lambda k, s, sl, bd: (0, 0, 0))
    grid_spec = pltpu.PrefetchScalarGridSpec(
        num_scalar_prefetch=2,
        grid=(fine_dev, stop_count),
        in_specs=[
            pl.BlockSpec(memory_space=pltpu.SMEM),
            whole,
            whole,
            whole,
            pl.BlockSpec((1, block_order, block_order), lambda k, s, sl, bd: (k, 0, 0)),
            pl.BlockSpec((1, block_order, column_count), lambda k, s, sl, bd: (k, 0, bd[0])),
        ],
        out_specs=pl.BlockSpec((1, 1, block_order, column_count), lambda k, s, sl, bd: (k, s, 0, 0)),
        scratch_shapes=[
            pltpu.VMEM((window_slots, block_order, column_count), jnp.float32),
            pltpu.VMEM((block_order, block_order), jnp.bfloat16),
        ],
    )
    hamiltonian = pl.pallas_call(
        kernel,
        grid_spec=grid_spec,
        out_shape=jax.ShapeDtypeStruct(
            (fine_dev, stop_count, block_order, column_count), jnp.bfloat16),
        compiler_params=pltpu.CompilerParams(
            dimension_semantics=("arbitrary", "arbitrary"), vmem_limit_bytes=48 * 1024 * 1024),
    )(slot_index, band_index, weights, before, coarse_kernel, after, intersection, intersection)
    partial_value = pl.pallas_call(
        functools.partial(product_kernel, stop_count=stop_count),
        grid=(fine_dev,),
        in_specs=[
            pl.BlockSpec((1, stop_count, block_order, column_count), lambda k: (k, 0, 0, 0)),
            pl.BlockSpec((stop_count, 1, column_count, vector_count), lambda k: (0, k, 0, 0)),
        ],
        out_specs=pl.BlockSpec((1, block_order, vector_count), lambda k: (k, 0, 0)),
        out_shape=jax.ShapeDtypeStruct((fine_dev, block_order, vector_count), jnp.bfloat16),
    )(hamiltonian, sources)
    product_share = lax.psum_scatter(partial_value, "band", scatter_dimension=1, tiled=True)
    return (hamiltonian, product_share)


def solution(mesh):
    placed = (
        P("blk", None, None),
        P("blk", None, None),
        P("blk", None, None),
        P(),
        P("blk", None, None),
        P("blk", "band", None),
    )
    return jax.shard_map(
        on_device,
        mesh=mesh,
        in_specs=placed,
        out_specs=(P("blk", None, None, "band"), P("blk", "band", None)),
        check_vma=False,
    )
```

```python
import functools

import jax
import jax.numpy as jnp
from jax import lax
from jax.experimental import pallas as pl
from jax.experimental.pallas import tpu as pltpu
from jax.sharding import PartitionSpec as P


def shifted(value, axis, steps):
    count = lax.axis_size(axis)
    pairs = [(source, (source + steps) % count) for source in range(count)]
    return lax.ppermute(value, axis, pairs)


def sandwich_kernel(slot_ref, band_ref, weight_ref, halo_ref, local_ref, inter_ref, right_ref,
                    ham_ref, prod_ref, rot_ref, *, blocks_dev, stop_count, corner_count):
    k = pl.program_id(0)
    column_count = right_ref.shape[2]
    right = right_ref[0]
    sources = [halo_ref.at[slot] for slot in range(blocks_dev)]
    sources += [local_ref.at[slot] for slot in range(blocks_dev)]
    sources += [halo_ref.at[blocks_dev + slot] for slot in range(blocks_dev)]
    for slot, source in enumerate(sources):
        prod_ref[slot] = jnp.dot(source[...], right, preferred_element_type=jnp.float32)
    for s in range(stop_count):
        base = (k * stop_count + s) * corner_count
        rotated = weight_ref[base] * prod_ref[slot_ref[base]]
        for j in range(1, corner_count):
            rotated = rotated + weight_ref[base + j] * prod_ref[slot_ref[base + j]]
        rot_ref[:, s * column_count:(s + 1) * column_count] = rotated.astype(jnp.bfloat16)
    left = inter_ref[0].T
    half = stop_count // 2
    for part in range(2):
        ham = jnp.dot(left, rot_ref[:, part * half * column_count:(part + 1) * half * column_count],
                      preferred_element_type=jnp.float32)
        for s in range(half):
            ham_ref[0, part * half + s] = ham[:, s * column_count:(s + 1) * column_count].astype(
                jnp.bfloat16)


def product_kernel(ham_ref, trial_ref, part_ref, *, stop_count):
    wide = jnp.concatenate([ham_ref[0, s] for s in range(stop_count)], axis=1)
    tall = jnp.concatenate([trial_ref[s, 0] for s in range(stop_count)], axis=0)
    part_ref[0] = jnp.dot(wide, tall, preferred_element_type=jnp.float32).astype(jnp.bfloat16)


def on_device(coarse_kernel, interp_index, interp_weight, stop_order, intersection, trial_vectors):
    blocks_dev = coarse_kernel.shape[0]
    fine_dev = intersection.shape[0]
    column_count = trial_vectors.shape[1]
    vector_count = trial_vectors.shape[2]
    block_order = intersection.shape[1]
    stop_count = stop_order.shape[0]
    corner_count = interp_index.shape[2]
    cycle_length = lax.axis_size("blk")
    total_coarse = blocks_dev * cycle_length
    position = lax.axis_index("blk")
    band = lax.axis_index("band")

    band_count = lax.axis_size("band")
    assert band_count == 2 * blocks_dev
    piece = lax.dynamic_index_in_dim(coarse_kernel, band % blocks_dev, 0, keepdims=True)
    pairs = []
    for i in range(cycle_length):
        for b in range(band_count):
            target = (i + 1) % cycle_length if b < blocks_dev else (i - 1) % cycle_length
            pairs.append((i * band_count + b, target * band_count + b))
    piece = lax.ppermute(piece, ("blk", "band"), pairs)
    halo = lax.all_gather(piece, "band", axis=0, tiled=True)
    halo, trial_vectors = lax.optimization_barrier((halo, trial_vectors))
    sources = jnp.stack(
        [shifted(trial_vectors, "blk", station + 1) for station in range(stop_count)])

    order_index = jnp.take(interp_index, stop_order, axis=1)
    order_weight = jnp.take(interp_weight, stop_order, axis=1)
    window_slots = 3 * blocks_dev
    local_index = jnp.mod(order_index - (position - 1) * blocks_dev, total_coarse)
    slot_group = local_index // blocks_dev
    slot_index = jnp.clip(slot_group, 0, 2) * blocks_dev + jnp.mod(local_index, blocks_dev)
    slot_index = jnp.clip(slot_index, 0, window_slots - 1).astype(jnp.int32).reshape(-1)
    weights = order_weight.astype(jnp.float32).reshape(-1)
    band_index = jnp.reshape(band, (1,)).astype(jnp.int32)

    kernel = functools.partial(
        sandwich_kernel, blocks_dev=blocks_dev, stop_count=stop_count, corner_count=corner_count)
    grid_spec = pltpu.PrefetchScalarGridSpec(
        num_scalar_prefetch=2,
        grid=(fine_dev,),
        in_specs=[
            pl.BlockSpec(memory_space=pltpu.SMEM),
            pl.BlockSpec((2 * blocks_dev, block_order, block_order), lambda k, sl, bd: (0, 0, 0)),
            pl.BlockSpec((blocks_dev, block_order, block_order), lambda k, sl, bd: (0, 0, 0)),
            pl.BlockSpec((1, block_order, block_order), lambda k, sl, bd: (k, 0, 0)),
            pl.BlockSpec((1, block_order, column_count), lambda k, sl, bd: (k, 0, bd[0])),
        ],
        out_specs=pl.BlockSpec(
            (1, stop_count, block_order, column_count), lambda k, sl, bd: (k, 0, 0, 0)),
        scratch_shapes=[
            pltpu.VMEM((window_slots, block_order, column_count), jnp.float32),
            pltpu.VMEM((block_order, stop_count * column_count), jnp.bfloat16),
        ],
    )
    hamiltonian = pl.pallas_call(
        kernel,
        grid_spec=grid_spec,
        out_shape=jax.ShapeDtypeStruct(
            (fine_dev, stop_count, block_order, column_count), jnp.bfloat16),
        compiler_params=pltpu.CompilerParams(
            dimension_semantics=("arbitrary",), vmem_limit_bytes=48 * 1024 * 1024),
    )(slot_index, band_index, weights, halo, coarse_kernel, intersection, intersection)
    partial_value = pl.pallas_call(
        functools.partial(product_kernel, stop_count=stop_count),
        grid=(fine_dev,),
        in_specs=[
            pl.BlockSpec((1, stop_count, block_order, column_count), lambda k: (k, 0, 0, 0)),
            pl.BlockSpec((stop_count, 1, column_count, vector_count), lambda k: (0, k, 0, 0)),
        ],
        out_specs=pl.BlockSpec((1, block_order, vector_count), lambda k: (k, 0, 0)),
        out_shape=jax.ShapeDtypeStruct((fine_dev, block_order, vector_count), jnp.bfloat16),
    )(hamiltonian, sources)
    product_share = lax.psum_scatter(partial_value, "band", scatter_dimension=1, tiled=True)
    return (hamiltonian, product_share)


def solution(mesh):
    placed = (
        P("blk", None, None),
        P("blk", None, None),
        P("blk", None, None),
        P(),
        P("blk", None, None),
        P("blk", "band", None),
    )
    return jax.shard_map(
        on_device,
        mesh=mesh,
        in_specs=placed,
        out_specs=(P("blk", None, None, "band"), P("blk", "band", None)),
        check_vma=False,
    )
```

```python
import functools

import jax
import jax.numpy as jnp
from jax import lax
from jax.experimental import pallas as pl
from jax.experimental.pallas import tpu as pltpu
from jax.sharding import PartitionSpec as P


def shifted(value, axis, steps):
    count = lax.axis_size(axis)
    pairs = [(source, (source + steps) % count) for source in range(count)]
    return lax.ppermute(value, axis, pairs)


def sandwich_kernel(slot_ref, band_ref, weight_ref, halo_ref, local_ref, inter_ref, right_ref,
                    ham_ref, prod_ref, rot_ref, *, blocks_dev, stop_count, corner_count):
    k = pl.program_id(0)
    column_count = right_ref.shape[2]
    right = right_ref[0]
    sources = [halo_ref.at[slot] for slot in range(blocks_dev)]
    sources += [local_ref.at[slot] for slot in range(blocks_dev)]
    sources += [halo_ref.at[blocks_dev + slot] for slot in range(blocks_dev)]
    for slot, source in enumerate(sources):
        prod_ref[slot] = jnp.dot(source[...], right, preferred_element_type=jnp.float32)
    for s in range(stop_count):
        base = (k * stop_count + s) * corner_count
        rotated = weight_ref[base] * prod_ref[slot_ref[base]]
        for j in range(1, corner_count):
            rotated = rotated + weight_ref[base + j] * prod_ref[slot_ref[base + j]]
        rot_ref[:, s * column_count:(s + 1) * column_count] = rotated.astype(jnp.bfloat16)
    left = inter_ref[0].T
    half = stop_count // 2
    for part in range(2):
        ham = jnp.dot(left, rot_ref[:, part * half * column_count:(part + 1) * half * column_count],
                      preferred_element_type=jnp.float32)
        for s in range(half):
            ham_ref[0, part * half + s] = ham[:, s * column_count:(s + 1) * column_count].astype(
                jnp.bfloat16)


def product_kernel(ham_ref, trial_ref, part_ref, *, stop_count):
    wide = jnp.concatenate([ham_ref[0, s] for s in range(stop_count)], axis=1)
    tall = jnp.concatenate([trial_ref[s, 0] for s in range(stop_count)], axis=0)
    part_ref[0] = jnp.dot(wide, tall, preferred_element_type=jnp.float32).astype(jnp.bfloat16)


def on_device(coarse_kernel, interp_index, interp_weight, stop_order, intersection, trial_vectors):
    blocks_dev = coarse_kernel.shape[0]
    fine_dev = intersection.shape[0]
    column_count = trial_vectors.shape[1]
    vector_count = trial_vectors.shape[2]
    block_order = intersection.shape[1]
    stop_count = stop_order.shape[0]
    corner_count = interp_index.shape[2]
    cycle_length = lax.axis_size("blk")
    total_coarse = blocks_dev * cycle_length
    position = lax.axis_index("blk")
    band = lax.axis_index("band")

    band_count = lax.axis_size("band")
    core = band % 2
    pairs = []
    for i in range(cycle_length):
        for b in range(band_count):
            target = (i + 1) % cycle_length if b % 2 == 0 else (i - 1) % cycle_length
            pairs.append((i * band_count + b, target * band_count + b))
    near = lax.ppermute(coarse_kernel, ("blk", "band"), pairs)
    far = lax.ppermute(near, "band", [(b, b ^ 1) for b in range(band_count)])
    halo = jnp.concatenate([near, far], axis=0)
    halo, trial_vectors = lax.optimization_barrier((halo, trial_vectors))
    sources = jnp.stack(
        [shifted(trial_vectors, "blk", station + 1) for station in range(stop_count)])

    order_index = jnp.take(interp_index, stop_order, axis=1)
    order_weight = jnp.take(interp_weight, stop_order, axis=1)
    window_slots = 3 * blocks_dev
    local_index = jnp.mod(order_index - (position - 1) * blocks_dev, total_coarse)
    slot_group = jnp.clip(local_index // blocks_dev, 0, 2)
    slot_group = jnp.where(core == 0, slot_group, 2 - slot_group)
    slot_index = slot_group * blocks_dev + jnp.mod(local_index, blocks_dev)
    slot_index = jnp.clip(slot_index, 0, window_slots - 1).astype(jnp.int32).reshape(-1)
    weights = order_weight.astype(jnp.float32).reshape(-1)
    band_index = jnp.reshape(band, (1,)).astype(jnp.int32)

    kernel = functools.partial(
        sandwich_kernel, blocks_dev=blocks_dev, stop_count=stop_count, corner_count=corner_count)
    grid_spec = pltpu.PrefetchScalarGridSpec(
        num_scalar_prefetch=2,
        grid=(fine_dev,),
        in_specs=[
            pl.BlockSpec(memory_space=pltpu.SMEM),
            pl.BlockSpec((2 * blocks_dev, block_order, block_order), lambda k, sl, bd: (0, 0, 0)),
            pl.BlockSpec((blocks_dev, block_order, block_order), lambda k, sl, bd: (0, 0, 0)),
            pl.BlockSpec((1, block_order, block_order), lambda k, sl, bd: (k, 0, 0)),
            pl.BlockSpec((1, block_order, column_count), lambda k, sl, bd: (k, 0, bd[0])),
        ],
        out_specs=pl.BlockSpec(
            (1, stop_count, block_order, column_count), lambda k, sl, bd: (k, 0, 0, 0)),
        scratch_shapes=[
            pltpu.VMEM((window_slots, block_order, column_count), jnp.float32),
            pltpu.VMEM((block_order, stop_count * column_count), jnp.bfloat16),
        ],
    )
    hamiltonian = pl.pallas_call(
        kernel,
        grid_spec=grid_spec,
        out_shape=jax.ShapeDtypeStruct(
            (fine_dev, stop_count, block_order, column_count), jnp.bfloat16),
        compiler_params=pltpu.CompilerParams(
            dimension_semantics=("arbitrary",), vmem_limit_bytes=48 * 1024 * 1024),
    )(slot_index, band_index, weights, halo, coarse_kernel, intersection, intersection)
    partial_value = pl.pallas_call(
        functools.partial(product_kernel, stop_count=stop_count),
        grid=(fine_dev,),
        in_specs=[
            pl.BlockSpec((1, stop_count, block_order, column_count), lambda k: (k, 0, 0, 0)),
            pl.BlockSpec((stop_count, 1, column_count, vector_count), lambda k: (0, k, 0, 0)),
        ],
        out_specs=pl.BlockSpec((1, block_order, vector_count), lambda k: (k, 0, 0)),
        out_shape=jax.ShapeDtypeStruct((fine_dev, block_order, vector_count), jnp.bfloat16),
    )(hamiltonian, sources)
    product_share = lax.psum_scatter(partial_value, "band", scatter_dimension=1, tiled=True)
    return (hamiltonian, product_share)


def solution(mesh):
    placed = (
        P("blk", None, None),
        P("blk", None, None),
        P("blk", None, None),
        P(),
        P("blk", None, None),
        P("blk", "band", None),
    )
    return jax.shard_map(
        on_device,
        mesh=mesh,
        in_specs=placed,
        out_specs=(P("blk", None, None, "band"), P("blk", "band", None)),
        check_vma=False,
    )
```

```python
import functools

import jax
import jax.numpy as jnp
from jax import lax
from jax.experimental import pallas as pl
from jax.experimental.pallas import tpu as pltpu
from jax.sharding import PartitionSpec as P


def shifted(value, axis, steps):
    count = lax.axis_size(axis)
    pairs = [(source, (source + steps) % count) for source in range(count)]
    return lax.ppermute(value, axis, pairs)


def sandwich_kernel(slot_ref, band_ref, weight_ref, halo_ref, local_ref, inter_ref, right_ref,
                    trial_ref, ham_ref, part_ref, prod_ref, rot_ref, wide_ref,
                    *, blocks_dev, stop_count, corner_count):
    k = pl.program_id(0)
    column_count = right_ref.shape[2]
    right = right_ref[0]
    sources = [halo_ref.at[slot] for slot in range(blocks_dev)]
    sources += [local_ref.at[slot] for slot in range(blocks_dev)]
    sources += [halo_ref.at[blocks_dev + slot] for slot in range(blocks_dev)]
    for slot, source in enumerate(sources):
        prod_ref[slot] = jnp.dot(source[...], right, preferred_element_type=jnp.float32)
    for s in range(stop_count):
        base = (k * stop_count + s) * corner_count
        rotated = weight_ref[base] * prod_ref[slot_ref[base]]
        for j in range(1, corner_count):
            rotated = rotated + weight_ref[base + j] * prod_ref[slot_ref[base + j]]
        rot_ref[:, s * column_count:(s + 1) * column_count] = rotated.astype(jnp.bfloat16)
    left = inter_ref[0].T
    half = stop_count // 2
    for part in range(2):
        ham = jnp.dot(left, rot_ref[:, part * half * column_count:(part + 1) * half * column_count],
                      preferred_element_type=jnp.float32)
        ham = ham.astype(jnp.bfloat16)
        wide_ref[:, part * half * column_count:(part + 1) * half * column_count] = ham
        for s in range(half):
            ham_ref[0, part * half + s] = ham[:, s * column_count:(s + 1) * column_count]
    tall = trial_ref[:, 0].reshape(stop_count * column_count, trial_ref.shape[3])
    part_ref[0] = jnp.dot(wide_ref[...], tall, preferred_element_type=jnp.float32).astype(
        jnp.bfloat16)


def on_device(coarse_kernel, interp_index, interp_weight, stop_order, intersection, trial_vectors):
    blocks_dev = coarse_kernel.shape[0]
    fine_dev = intersection.shape[0]
    column_count = trial_vectors.shape[1]
    vector_count = trial_vectors.shape[2]
    block_order = intersection.shape[1]
    stop_count = stop_order.shape[0]
    corner_count = interp_index.shape[2]
    cycle_length = lax.axis_size("blk")
    total_coarse = blocks_dev * cycle_length
    position = lax.axis_index("blk")
    band = lax.axis_index("band")

    band_count = lax.axis_size("band")
    core = band % 2
    pairs = []
    for i in range(cycle_length):
        for b in range(band_count):
            target = (i + 1) % cycle_length if b % 2 == 0 else (i - 1) % cycle_length
            pairs.append((i * band_count + b, target * band_count + b))
    near = lax.ppermute(coarse_kernel, ("blk", "band"), pairs)
    far = lax.ppermute(near, "band", [(b, b ^ 1) for b in range(band_count)])
    halo = jnp.concatenate([near, far], axis=0)
    sources = jnp.stack(
        [shifted(trial_vectors, "blk", station + 1) for station in range(stop_count)])

    order_index = jnp.take(interp_index, stop_order, axis=1)
    order_weight = jnp.take(interp_weight, stop_order, axis=1)
    window_slots = 3 * blocks_dev
    local_index = jnp.mod(order_index - (position - 1) * blocks_dev, total_coarse)
    slot_group = jnp.clip(local_index // blocks_dev, 0, 2)
    slot_group = jnp.where(core == 0, slot_group, 2 - slot_group)
    slot_index = slot_group * blocks_dev + jnp.mod(local_index, blocks_dev)
    slot_index = jnp.clip(slot_index, 0, window_slots - 1).astype(jnp.int32).reshape(-1)
    weights = order_weight.astype(jnp.float32).reshape(-1)
    band_index = jnp.reshape(band, (1,)).astype(jnp.int32)

    kernel = functools.partial(
        sandwich_kernel, blocks_dev=blocks_dev, stop_count=stop_count, corner_count=corner_count)
    grid_spec = pltpu.PrefetchScalarGridSpec(
        num_scalar_prefetch=2,
        grid=(fine_dev,),
        in_specs=[
            pl.BlockSpec(memory_space=pltpu.SMEM),
            pl.BlockSpec((2 * blocks_dev, block_order, block_order), lambda k, sl, bd: (0, 0, 0)),
            pl.BlockSpec((blocks_dev, block_order, block_order), lambda k, sl, bd: (0, 0, 0)),
            pl.BlockSpec((1, block_order, block_order), lambda k, sl, bd: (k, 0, 0)),
            pl.BlockSpec((1, block_order, column_count), lambda k, sl, bd: (k, 0, bd[0])),
            pl.BlockSpec(
                (stop_count, 1, column_count, vector_count), lambda k, sl, bd: (0, k, 0, 0)),
        ],
        out_specs=[
            pl.BlockSpec(
                (1, stop_count, block_order, column_count), lambda k, sl, bd: (k, 0, 0, 0)),
            pl.BlockSpec((1, block_order, vector_count), lambda k, sl, bd: (k, 0, 0)),
        ],
        scratch_shapes=[
            pltpu.VMEM((window_slots, block_order, column_count), jnp.float32),
            pltpu.VMEM((block_order, stop_count * column_count), jnp.bfloat16),
            pltpu.VMEM((block_order, stop_count * column_count), jnp.bfloat16),
        ],
    )
    hamiltonian, partial_value = pl.pallas_call(
        kernel,
        grid_spec=grid_spec,
        out_shape=[
            jax.ShapeDtypeStruct((fine_dev, stop_count, block_order, column_count), jnp.bfloat16),
            jax.ShapeDtypeStruct((fine_dev, block_order, vector_count), jnp.bfloat16),
        ],
        compiler_params=pltpu.CompilerParams(
            dimension_semantics=("arbitrary",), vmem_limit_bytes=48 * 1024 * 1024),
    )(slot_index, band_index, weights, halo, coarse_kernel, intersection, intersection, sources)
    product_share = lax.psum_scatter(partial_value, "band", scatter_dimension=1, tiled=True)
    return (hamiltonian, product_share)


def solution(mesh):
    placed = (
        P("blk", None, None),
        P("blk", None, None),
        P("blk", None, None),
        P(),
        P("blk", None, None),
        P("blk", "band", None),
    )
    return jax.shard_map(
        on_device,
        mesh=mesh,
        in_specs=placed,
        out_specs=(P("blk", None, None, "band"), P("blk", "band", None)),
        check_vma=False,
    )
```

```python
import functools

import jax
import jax.numpy as jnp
from jax import lax
from jax.experimental import pallas as pl
from jax.experimental.pallas import tpu as pltpu
from jax.sharding import PartitionSpec as P


def shifted(value, axis, steps):
    count = lax.axis_size(axis)
    pairs = [(source, (source + steps) % count) for source in range(count)]
    return lax.ppermute(value, axis, pairs)


def sandwich_kernel(slot_ref, band_ref, weight_ref, halo_ref, local_ref, inter_ref, right_ref,
                    trial_ref, ham_ref, part_ref, prod_ref, rot_ref, wide_ref,
                    *, blocks_dev, stop_count, corner_count):
    k = pl.program_id(0)
    column_count = right_ref.shape[2]
    right = right_ref[0]
    sources = [halo_ref.at[slot] for slot in range(blocks_dev)]
    sources += [local_ref.at[slot] for slot in range(blocks_dev)]
    sources += [halo_ref.at[blocks_dev + slot] for slot in range(blocks_dev)]
    for slot, source in enumerate(sources):
        prod_ref[slot] = jnp.dot(source[...], right, preferred_element_type=jnp.float32)
    for s in range(stop_count):
        base = (k * stop_count + s) * corner_count
        rotated = weight_ref[base] * prod_ref[slot_ref[base]]
        for j in range(1, corner_count):
            rotated = rotated + weight_ref[base + j] * prod_ref[slot_ref[base + j]]
        rot_ref[:, s * column_count:(s + 1) * column_count] = rotated.astype(jnp.bfloat16)
    left = inter_ref[0].T
    half = stop_count // 2
    for part in range(2):
        ham = jnp.dot(left, rot_ref[:, part * half * column_count:(part + 1) * half * column_count],
                      preferred_element_type=jnp.float32)
        ham = ham.astype(jnp.bfloat16)
        wide_ref[:, part * half * column_count:(part + 1) * half * column_count] = ham
        for s in range(half):
            ham_ref[0, part * half + s] = ham[:, s * column_count:(s + 1) * column_count]
    tall = trial_ref[:, 0].reshape(stop_count * column_count, trial_ref.shape[3])
    part_ref[0] = jnp.dot(wide_ref[...], tall, preferred_element_type=jnp.float32)


def on_device(coarse_kernel, interp_index, interp_weight, stop_order, intersection, trial_vectors):
    blocks_dev = coarse_kernel.shape[0]
    fine_dev = intersection.shape[0]
    column_count = trial_vectors.shape[1]
    vector_count = trial_vectors.shape[2]
    block_order = intersection.shape[1]
    stop_count = stop_order.shape[0]
    corner_count = interp_index.shape[2]
    cycle_length = lax.axis_size("blk")
    total_coarse = blocks_dev * cycle_length
    position = lax.axis_index("blk")
    band = lax.axis_index("band")

    band_count = lax.axis_size("band")
    core = band % 2
    pairs = []
    for i in range(cycle_length):
        for b in range(band_count):
            target = (i + 1) % cycle_length if b % 2 == 0 else (i - 1) % cycle_length
            pairs.append((i * band_count + b, target * band_count + b))
    near = lax.ppermute(coarse_kernel, ("blk", "band"), pairs)
    far = lax.ppermute(near, "band", [(b, b ^ 1) for b in range(band_count)])
    halo = jnp.concatenate([near, far], axis=0)
    sources = jnp.stack(
        [shifted(trial_vectors, "blk", station + 1) for station in range(stop_count)])

    order_index = jnp.take(interp_index, stop_order, axis=1)
    order_weight = jnp.take(interp_weight, stop_order, axis=1)
    window_slots = 3 * blocks_dev
    local_index = jnp.mod(order_index - (position - 1) * blocks_dev, total_coarse)
    slot_group = jnp.clip(local_index // blocks_dev, 0, 2)
    slot_group = jnp.where(core == 0, slot_group, 2 - slot_group)
    slot_index = slot_group * blocks_dev + jnp.mod(local_index, blocks_dev)
    slot_index = jnp.clip(slot_index, 0, window_slots - 1).astype(jnp.int32).reshape(-1)
    weights = order_weight.astype(jnp.float32).reshape(-1)
    band_index = jnp.reshape(band, (1,)).astype(jnp.int32)

    kernel = functools.partial(
        sandwich_kernel, blocks_dev=blocks_dev, stop_count=stop_count, corner_count=corner_count)
    grid_spec = pltpu.PrefetchScalarGridSpec(
        num_scalar_prefetch=2,
        grid=(fine_dev,),
        in_specs=[
            pl.BlockSpec(memory_space=pltpu.SMEM),
            pl.BlockSpec((2 * blocks_dev, block_order, block_order), lambda k, sl, bd: (0, 0, 0)),
            pl.BlockSpec((blocks_dev, block_order, block_order), lambda k, sl, bd: (0, 0, 0)),
            pl.BlockSpec((1, block_order, block_order), lambda k, sl, bd: (k, 0, 0)),
            pl.BlockSpec((1, block_order, column_count), lambda k, sl, bd: (k, 0, bd[0])),
            pl.BlockSpec(
                (stop_count, 1, column_count, vector_count), lambda k, sl, bd: (0, k, 0, 0)),
        ],
        out_specs=[
            pl.BlockSpec(
                (1, stop_count, block_order, column_count), lambda k, sl, bd: (k, 0, 0, 0)),
            pl.BlockSpec((1, block_order, vector_count), lambda k, sl, bd: (k, 0, 0)),
        ],
        scratch_shapes=[
            pltpu.VMEM((window_slots, block_order, column_count), jnp.float32),
            pltpu.VMEM((block_order, stop_count * column_count), jnp.bfloat16),
            pltpu.VMEM((block_order, stop_count * column_count), jnp.bfloat16),
        ],
    )
    hamiltonian, partial_value = pl.pallas_call(
        kernel,
        grid_spec=grid_spec,
        out_shape=[
            jax.ShapeDtypeStruct((fine_dev, stop_count, block_order, column_count), jnp.bfloat16),
            jax.ShapeDtypeStruct((fine_dev, block_order, vector_count), jnp.float32),
        ],
        compiler_params=pltpu.CompilerParams(
            dimension_semantics=("arbitrary",), vmem_limit_bytes=48 * 1024 * 1024),
    )(slot_index, band_index, weights, halo, coarse_kernel, intersection, intersection, sources)
    row_block = block_order // band_count
    halves = partial_value.reshape(fine_dev, 2, 2, row_block, vector_count)
    send = lax.dynamic_index_in_dim(halves, 1 - core, 2, keepdims=False)
    keep = lax.dynamic_index_in_dim(halves, core, 2, keepdims=False)
    swap = [(b, b ^ 1) for b in range(band_count)]
    pair_sum = keep + lax.ppermute(send.astype(jnp.bfloat16), "band", swap).astype(jnp.float32)
    level = band // 2
    send = lax.dynamic_index_in_dim(pair_sum, 1 - level, 1, keepdims=False)
    keep = lax.dynamic_index_in_dim(pair_sum, level, 1, keepdims=False)
    swap = [(b, b ^ 2) for b in range(band_count)]
    product_share = (
        keep + lax.ppermute(send.astype(jnp.bfloat16), "band", swap).astype(jnp.float32)
    ).astype(jnp.bfloat16)
    return (hamiltonian, product_share)


def solution(mesh):
    placed = (
        P("blk", None, None),
        P("blk", None, None),
        P("blk", None, None),
        P(),
        P("blk", None, None),
        P("blk", "band", None),
    )
    return jax.shard_map(
        on_device,
        mesh=mesh,
        in_specs=placed,
        out_specs=(P("blk", None, None, "band"), P("blk", "band", None)),
        check_vma=False,
    )
```

```python
import functools

import jax
import jax.numpy as jnp
from jax import lax
from jax.experimental import pallas as pl
from jax.experimental.pallas import tpu as pltpu
from jax.sharding import PartitionSpec as P


def shifted(value, axis, steps):
    count = lax.axis_size(axis)
    pairs = [(source, (source + steps) % count) for source in range(count)]
    return lax.ppermute(value, axis, pairs)


def sandwich_kernel(slot_ref, band_ref, weight_ref, halo_ref, local_ref, inter_ref, right_ref,
                    ham_ref, prod_ref, rot_ref, *, blocks_dev, stop_count, corner_count):
    k = pl.program_id(0)
    column_count = right_ref.shape[2]
    right = right_ref[0]
    sources = [halo_ref.at[slot] for slot in range(blocks_dev)]
    sources += [local_ref.at[slot] for slot in range(blocks_dev)]
    sources += [halo_ref.at[blocks_dev + slot] for slot in range(blocks_dev)]
    for slot, source in enumerate(sources):
        prod_ref[slot] = jnp.dot(source[...], right, preferred_element_type=jnp.float32)
    for s in range(stop_count):
        base = (k * stop_count + s) * corner_count
        rotated = weight_ref[base] * prod_ref[slot_ref[base]]
        for j in range(1, corner_count):
            rotated = rotated + weight_ref[base + j] * prod_ref[slot_ref[base + j]]
        rot_ref[:, s * column_count:(s + 1) * column_count] = rotated.astype(jnp.bfloat16)
    left = inter_ref[0].T
    half = stop_count // 2
    for part in range(2):
        ham = jnp.dot(left, rot_ref[:, part * half * column_count:(part + 1) * half * column_count],
                      preferred_element_type=jnp.float32)
        ham = ham.astype(jnp.bfloat16)
        for s in range(half):
            ham_ref[0, part * half + s] = ham[:, s * column_count:(s + 1) * column_count]


def product_kernel(ham_ref, *refs, stop_count):
    trial_refs, part_ref = refs[:stop_count], refs[stop_count]
    wide = jnp.concatenate([ham_ref[0, s] for s in range(stop_count)], axis=1)
    tall = jnp.concatenate([trial_refs[s][0] for s in range(stop_count)], axis=0)
    part_ref[0] = jnp.dot(wide, tall, preferred_element_type=jnp.float32)


def on_device(coarse_kernel, interp_index, interp_weight, stop_order, intersection, trial_vectors):
    blocks_dev = coarse_kernel.shape[0]
    fine_dev = intersection.shape[0]
    column_count = trial_vectors.shape[1]
    vector_count = trial_vectors.shape[2]
    block_order = intersection.shape[1]
    stop_count = stop_order.shape[0]
    corner_count = interp_index.shape[2]
    cycle_length = lax.axis_size("blk")
    total_coarse = blocks_dev * cycle_length
    position = lax.axis_index("blk")
    band = lax.axis_index("band")

    band_count = lax.axis_size("band")
    core = band % 2
    pairs = []
    for i in range(cycle_length):
        for b in range(band_count):
            target = (i + 1) % cycle_length if b % 2 == 0 else (i - 1) % cycle_length
            pairs.append((i * band_count + b, target * band_count + b))
    near = lax.ppermute(coarse_kernel, ("blk", "band"), pairs)
    far = lax.ppermute(near, "band", [(b, b ^ 1) for b in range(band_count)])
    halo = jnp.concatenate([near, far], axis=0)
    sources = [shifted(trial_vectors, "blk", station + 1) for station in range(stop_count)]

    order_index = jnp.take(interp_index, stop_order, axis=1)
    order_weight = jnp.take(interp_weight, stop_order, axis=1)
    window_slots = 3 * blocks_dev
    local_index = jnp.mod(order_index - (position - 1) * blocks_dev, total_coarse)
    slot_group = jnp.clip(local_index // blocks_dev, 0, 2)
    slot_group = jnp.where(core == 0, slot_group, 2 - slot_group)
    slot_index = slot_group * blocks_dev + jnp.mod(local_index, blocks_dev)
    slot_index = jnp.clip(slot_index, 0, window_slots - 1).astype(jnp.int32).reshape(-1)
    weights = order_weight.astype(jnp.float32).reshape(-1)
    band_index = jnp.reshape(band, (1,)).astype(jnp.int32)

    kernel = functools.partial(
        sandwich_kernel, blocks_dev=blocks_dev, stop_count=stop_count, corner_count=corner_count)
    grid_spec = pltpu.PrefetchScalarGridSpec(
        num_scalar_prefetch=2,
        grid=(fine_dev,),
        in_specs=[
            pl.BlockSpec(memory_space=pltpu.SMEM),
            pl.BlockSpec((2 * blocks_dev, block_order, block_order), lambda k, sl, bd: (0, 0, 0)),
            pl.BlockSpec((blocks_dev, block_order, block_order), lambda k, sl, bd: (0, 0, 0)),
            pl.BlockSpec((1, block_order, block_order), lambda k, sl, bd: (k, 0, 0)),
            pl.BlockSpec((1, block_order, column_count), lambda k, sl, bd: (k, 0, bd[0])),
        ],
        out_specs=pl.BlockSpec(
            (1, stop_count, block_order, column_count), lambda k, sl, bd: (k, 0, 0, 0)),
        scratch_shapes=[
            pltpu.VMEM((window_slots, block_order, column_count), jnp.float32),
            pltpu.VMEM((block_order, stop_count * column_count), jnp.bfloat16),
        ],
    )
    hamiltonian = pl.pallas_call(
        kernel,
        grid_spec=grid_spec,
        out_shape=jax.ShapeDtypeStruct(
            (fine_dev, stop_count, block_order, column_count), jnp.bfloat16),
        compiler_params=pltpu.CompilerParams(
            dimension_semantics=("arbitrary",), vmem_limit_bytes=48 * 1024 * 1024),
        cost_estimate=pl.CostEstimate(
            flops=2 * fine_dev * block_order * block_order * column_count * (window_slots + stop_count),
            transcendentals=0,
            bytes_accessed=2 * fine_dev * block_order * (block_order + stop_count * column_count)),
    )(slot_index, band_index, weights, halo, coarse_kernel, intersection, intersection)
    partial_value = pl.pallas_call(
        functools.partial(product_kernel, stop_count=stop_count),
        grid=(fine_dev,),
        in_specs=[
            pl.BlockSpec((1, stop_count, block_order, column_count), lambda k: (k, 0, 0, 0)),
        ] + [pl.BlockSpec((1, column_count, vector_count), lambda k: (k, 0, 0))] * stop_count,
        out_specs=pl.BlockSpec((1, block_order, vector_count), lambda k: (k, 0, 0)),
        out_shape=jax.ShapeDtypeStruct((fine_dev, block_order, vector_count), jnp.float32),
        cost_estimate=pl.CostEstimate(
            flops=2 * fine_dev * stop_count * block_order * column_count * vector_count,
            transcendentals=0,
            bytes_accessed=2 * fine_dev * stop_count * block_order * column_count),
    )(hamiltonian, *sources)
    row_block = block_order // band_count
    halves = partial_value.reshape(fine_dev, 2, 2, row_block, vector_count)
    send = lax.dynamic_index_in_dim(halves, 1 - core, 2, keepdims=False)
    keep = lax.dynamic_index_in_dim(halves, core, 2, keepdims=False)
    swap = [(b, b ^ 1) for b in range(band_count)]
    pair_sum = keep + lax.ppermute(send.astype(jnp.bfloat16), "band", swap).astype(jnp.float32)
    level = band // 2
    send = lax.dynamic_index_in_dim(pair_sum, 1 - level, 1, keepdims=False)
    keep = lax.dynamic_index_in_dim(pair_sum, level, 1, keepdims=False)
    swap = [(b, b ^ 2) for b in range(band_count)]
    product_share = (
        keep + lax.ppermute(send.astype(jnp.bfloat16), "band", swap).astype(jnp.float32)
    ).astype(jnp.bfloat16)
    return (hamiltonian, product_share)


def solution(mesh):
    placed = (
        P("blk", None, None),
        P("blk", None, None),
        P("blk", None, None),
        P(),
        P("blk", None, None),
        P("blk", "band", None),
    )
    return jax.shard_map(
        on_device,
        mesh=mesh,
        in_specs=placed,
        out_specs=(P("blk", None, None, "band"), P("blk", "band", None)),
        check_vma=False,
    )
```

```python
import functools

import jax
import jax.numpy as jnp
from jax import lax
from jax.experimental import pallas as pl
from jax.experimental.pallas import tpu as pltpu
from jax.sharding import PartitionSpec as P


def shifted(value, axis, steps):
    count = lax.axis_size(axis)
    pairs = [(source, (source + steps) % count) for source in range(count)]
    return lax.ppermute(value, axis, pairs)


def sandwich_kernel(slot_ref, band_ref, weight_ref, halo_ref, local_ref, inter_ref, right_ref,
                    ham_ref, prod_ref, rot_ref, *, blocks_dev, stop_count, corner_count):
    k = pl.program_id(0)
    column_count = right_ref.shape[2]
    right = right_ref[0]
    sources = [halo_ref.at[slot] for slot in range(blocks_dev)]
    sources += [local_ref.at[slot] for slot in range(blocks_dev)]
    sources += [halo_ref.at[blocks_dev + slot] for slot in range(blocks_dev)]
    for slot, source in enumerate(sources):
        prod_ref[slot] = jnp.dot(source[...], right, preferred_element_type=jnp.float32)
    for s in range(stop_count):
        base = (k * stop_count + s) * corner_count
        rotated = weight_ref[base] * prod_ref[slot_ref[base]]
        for j in range(1, corner_count):
            rotated = rotated + weight_ref[base + j] * prod_ref[slot_ref[base + j]]
        rot_ref[:, s * column_count:(s + 1) * column_count] = rotated.astype(jnp.bfloat16)
    left = inter_ref[0].T
    half = stop_count // 2
    for part in range(2):
        ham = jnp.dot(left, rot_ref[:, part * half * column_count:(part + 1) * half * column_count],
                      preferred_element_type=jnp.float32)
        ham = ham.astype(jnp.bfloat16)
        for s in range(half):
            ham_ref[0, part * half + s] = ham[:, s * column_count:(s + 1) * column_count]


def product_kernel(ham_ref, *refs, stop_count):
    trial_refs, part_ref = refs[:stop_count], refs[stop_count]
    wide = jnp.concatenate([ham_ref[0, s] for s in range(stop_count)], axis=1)
    tall = jnp.concatenate([trial_refs[s][0] for s in range(stop_count)], axis=0)
    part_ref[0] = jnp.dot(wide, tall, preferred_element_type=jnp.float32)


def on_device(coarse_kernel, interp_index, interp_weight, stop_order, intersection, trial_vectors):
    blocks_dev = coarse_kernel.shape[0]
    fine_dev = intersection.shape[0]
    column_count = trial_vectors.shape[1]
    vector_count = trial_vectors.shape[2]
    block_order = intersection.shape[1]
    stop_count = stop_order.shape[0]
    corner_count = interp_index.shape[2]
    cycle_length = lax.axis_size("blk")
    total_coarse = blocks_dev * cycle_length
    position = lax.axis_index("blk")
    band = lax.axis_index("band")

    band_count = lax.axis_size("band")
    core = band % 2
    pairs = []
    for i in range(cycle_length):
        for b in range(band_count):
            target = (i + 1) % cycle_length if b % 2 == 0 else (i - 1) % cycle_length
            pairs.append((i * band_count + b, target * band_count + (b ^ 2)))
    near = lax.ppermute(coarse_kernel, ("blk", "band"), pairs)
    far = lax.ppermute(near, "band", [(b, b ^ 1) for b in range(band_count)])
    halo = jnp.concatenate([near, far], axis=0)
    sources = [shifted(trial_vectors, "blk", station + 1) for station in range(stop_count)]

    order_index = jnp.take(interp_index, stop_order, axis=1)
    order_weight = jnp.take(interp_weight, stop_order, axis=1)
    window_slots = 3 * blocks_dev
    local_index = jnp.mod(order_index - (position - 1) * blocks_dev, total_coarse)
    slot_group = jnp.clip(local_index // blocks_dev, 0, 2)
    slot_group = jnp.where(core == 0, slot_group, 2 - slot_group)
    slot_index = slot_group * blocks_dev + jnp.mod(local_index, blocks_dev)
    slot_index = jnp.clip(slot_index, 0, window_slots - 1).astype(jnp.int32).reshape(-1)
    weights = order_weight.astype(jnp.float32).reshape(-1)
    band_index = jnp.reshape(band, (1,)).astype(jnp.int32)

    kernel = functools.partial(
        sandwich_kernel, blocks_dev=blocks_dev, stop_count=stop_count, corner_count=corner_count)
    grid_spec = pltpu.PrefetchScalarGridSpec(
        num_scalar_prefetch=2,
        grid=(fine_dev,),
        in_specs=[
            pl.BlockSpec(memory_space=pltpu.SMEM),
            pl.BlockSpec((2 * blocks_dev, block_order, block_order), lambda k, sl, bd: (0, 0, 0)),
            pl.BlockSpec((blocks_dev, block_order, block_order), lambda k, sl, bd: (0, 0, 0)),
            pl.BlockSpec((1, block_order, block_order), lambda k, sl, bd: (k, 0, 0)),
            pl.BlockSpec((1, block_order, column_count), lambda k, sl, bd: (k, 0, bd[0])),
        ],
        out_specs=pl.BlockSpec(
            (1, stop_count, block_order, column_count), lambda k, sl, bd: (k, 0, 0, 0)),
        scratch_shapes=[
            pltpu.VMEM((window_slots, block_order, column_count), jnp.float32),
            pltpu.VMEM((block_order, stop_count * column_count), jnp.bfloat16),
        ],
    )
    hamiltonian = pl.pallas_call(
        kernel,
        grid_spec=grid_spec,
        out_shape=jax.ShapeDtypeStruct(
            (fine_dev, stop_count, block_order, column_count), jnp.bfloat16),
        compiler_params=pltpu.CompilerParams(
            dimension_semantics=("arbitrary",), vmem_limit_bytes=48 * 1024 * 1024),
        cost_estimate=pl.CostEstimate(
            flops=2 * fine_dev * block_order * block_order * column_count * (window_slots + stop_count),
            transcendentals=0,
            bytes_accessed=2 * fine_dev * block_order * (block_order + stop_count * column_count)),
    )(slot_index, band_index, weights, halo, coarse_kernel, intersection, intersection)
    partial_value = pl.pallas_call(
        functools.partial(product_kernel, stop_count=stop_count),
        grid=(fine_dev,),
        in_specs=[
            pl.BlockSpec((1, stop_count, block_order, column_count), lambda k: (k, 0, 0, 0)),
        ] + [pl.BlockSpec((1, column_count, vector_count), lambda k: (k, 0, 0))] * stop_count,
        out_specs=pl.BlockSpec((1, block_order, vector_count), lambda k: (k, 0, 0)),
        out_shape=jax.ShapeDtypeStruct((fine_dev, block_order, vector_count), jnp.float32),
        cost_estimate=pl.CostEstimate(
            flops=2 * fine_dev * stop_count * block_order * column_count * vector_count,
            transcendentals=0,
            bytes_accessed=2 * fine_dev * stop_count * block_order * column_count),
    )(hamiltonian, *sources)
    row_block = block_order // band_count
    halves = partial_value.reshape(fine_dev, 2, 2, row_block, vector_count)
    send = lax.dynamic_index_in_dim(halves, 1 - core, 2, keepdims=False)
    keep = lax.dynamic_index_in_dim(halves, core, 2, keepdims=False)
    swap = [(b, b ^ 1) for b in range(band_count)]
    pair_sum = keep + lax.ppermute(send.astype(jnp.bfloat16), "band", swap).astype(jnp.float32)
    level = band // 2
    send = lax.dynamic_index_in_dim(pair_sum, 1 - level, 1, keepdims=False)
    keep = lax.dynamic_index_in_dim(pair_sum, level, 1, keepdims=False)
    swap = [(b, b ^ 2) for b in range(band_count)]
    product_share = (
        keep + lax.ppermute(send.astype(jnp.bfloat16), "band", swap).astype(jnp.float32)
    ).astype(jnp.bfloat16)
    return (hamiltonian, product_share)


def solution(mesh):
    placed = (
        P("blk", None, None),
        P("blk", None, None),
        P("blk", None, None),
        P(),
        P("blk", None, None),
        P("blk", "band", None),
    )
    return jax.shard_map(
        on_device,
        mesh=mesh,
        in_specs=placed,
        out_specs=(P("blk", None, None, "band"), P("blk", "band", None)),
        check_vma=False,
    )
```

```python
import functools

import jax
import jax.numpy as jnp
from jax import lax
from jax.experimental import pallas as pl
from jax.experimental.pallas import tpu as pltpu
from jax.sharding import PartitionSpec as P


def shifted(value, axis, steps):
    count = lax.axis_size(axis)
    pairs = [(source, (source + steps) % count) for source in range(count)]
    return lax.ppermute(value, axis, pairs)


def sandwich_kernel(slot_ref, band_ref, weight_ref, halo_ref, local_ref, inter_ref, right_ref,
                    ham_ref, prod_ref, rot_ref, *, blocks_dev, stop_count, corner_count):
    k = pl.program_id(0)
    column_count = right_ref.shape[2]
    right = right_ref[0]
    sources = [halo_ref.at[slot] for slot in range(blocks_dev)]
    sources += [local_ref.at[slot] for slot in range(blocks_dev)]
    sources += [halo_ref.at[blocks_dev + slot] for slot in range(blocks_dev)]
    for slot, source in enumerate(sources):
        prod_ref[slot] = jnp.dot(source[...], right, preferred_element_type=jnp.float32)
    for s in range(stop_count):
        base = (k * stop_count + s) * corner_count
        rotated = weight_ref[base] * prod_ref[slot_ref[base]]
        for j in range(1, corner_count):
            rotated = rotated + weight_ref[base + j] * prod_ref[slot_ref[base + j]]
        rot_ref[:, s * column_count:(s + 1) * column_count] = rotated.astype(jnp.bfloat16)
    left = inter_ref[0].T
    half = stop_count // 2
    for part in range(2):
        ham = jnp.dot(left, rot_ref[:, part * half * column_count:(part + 1) * half * column_count],
                      preferred_element_type=jnp.float32)
        ham = ham.astype(jnp.bfloat16)
        for s in range(half):
            ham_ref[0, part * half + s] = ham[:, s * column_count:(s + 1) * column_count]


def product_kernel(ham_ref, *refs, stop_count):
    trial_refs, part_ref = refs[:stop_count], refs[stop_count]
    wide = jnp.concatenate([ham_ref[0, s] for s in range(stop_count)], axis=1)
    tall = jnp.concatenate([trial_refs[s][0] for s in range(stop_count)], axis=0)
    part_ref[0] = jnp.dot(wide, tall, preferred_element_type=jnp.float32)


def on_device(coarse_kernel, interp_index, interp_weight, stop_order, intersection, trial_vectors):
    blocks_dev = coarse_kernel.shape[0]
    fine_dev = intersection.shape[0]
    column_count = trial_vectors.shape[1]
    vector_count = trial_vectors.shape[2]
    block_order = intersection.shape[1]
    stop_count = stop_order.shape[0]
    corner_count = interp_index.shape[2]
    cycle_length = lax.axis_size("blk")
    total_coarse = blocks_dev * cycle_length
    position = lax.axis_index("blk")
    band = lax.axis_index("band")

    band_count = lax.axis_size("band")
    core = band % 2
    pairs = []
    for i in range(cycle_length):
        for b in range(band_count):
            target = (i + 1) % cycle_length if b % 2 == 0 else (i - 1) % cycle_length
            pairs.append((i * band_count + b, target * band_count + b))
    near = lax.ppermute(coarse_kernel, ("blk", "band"), pairs)
    far = lax.ppermute(near, "band", [(b, b ^ 1) for b in range(band_count)])
    halo = jnp.concatenate([near, far], axis=0)
    assert stop_count == 8
    first = shifted(trial_vectors, "blk", 1)
    last = shifted(trial_vectors, "blk", 8)
    second = shifted(jnp.stack([trial_vectors, first]), "blk", 2)
    third = shifted(jnp.stack([trial_vectors, first, second[0], second[1]]), "blk", 4)
    sources = [first, second[0], second[1], third[0], third[1], third[2], third[3], last]

    order_index = jnp.take(interp_index, stop_order, axis=1)
    order_weight = jnp.take(interp_weight, stop_order, axis=1)
    window_slots = 3 * blocks_dev
    local_index = jnp.mod(order_index - (position - 1) * blocks_dev, total_coarse)
    slot_group = jnp.clip(local_index // blocks_dev, 0, 2)
    slot_group = jnp.where(core == 0, slot_group, 2 - slot_group)
    slot_index = slot_group * blocks_dev + jnp.mod(local_index, blocks_dev)
    slot_index = jnp.clip(slot_index, 0, window_slots - 1).astype(jnp.int32).reshape(-1)
    weights = order_weight.astype(jnp.float32).reshape(-1)
    band_index = jnp.reshape(band, (1,)).astype(jnp.int32)

    kernel = functools.partial(
        sandwich_kernel, blocks_dev=blocks_dev, stop_count=stop_count, corner_count=corner_count)
    grid_spec = pltpu.PrefetchScalarGridSpec(
        num_scalar_prefetch=2,
        grid=(fine_dev,),
        in_specs=[
            pl.BlockSpec(memory_space=pltpu.SMEM),
            pl.BlockSpec((2 * blocks_dev, block_order, block_order), lambda k, sl, bd: (0, 0, 0)),
            pl.BlockSpec((blocks_dev, block_order, block_order), lambda k, sl, bd: (0, 0, 0)),
            pl.BlockSpec((1, block_order, block_order), lambda k, sl, bd: (k, 0, 0)),
            pl.BlockSpec((1, block_order, column_count), lambda k, sl, bd: (k, 0, bd[0])),
        ],
        out_specs=pl.BlockSpec(
            (1, stop_count, block_order, column_count), lambda k, sl, bd: (k, 0, 0, 0)),
        scratch_shapes=[
            pltpu.VMEM((window_slots, block_order, column_count), jnp.float32),
            pltpu.VMEM((block_order, stop_count * column_count), jnp.bfloat16),
        ],
    )
    hamiltonian = pl.pallas_call(
        kernel,
        grid_spec=grid_spec,
        out_shape=jax.ShapeDtypeStruct(
            (fine_dev, stop_count, block_order, column_count), jnp.bfloat16),
        compiler_params=pltpu.CompilerParams(
            dimension_semantics=("arbitrary",), vmem_limit_bytes=48 * 1024 * 1024),
        cost_estimate=pl.CostEstimate(
            flops=2 * fine_dev * block_order * block_order * column_count * (window_slots + stop_count),
            transcendentals=0,
            bytes_accessed=2 * fine_dev * block_order * (block_order + stop_count * column_count)),
    )(slot_index, band_index, weights, halo, coarse_kernel, intersection, intersection)
    partial_value = pl.pallas_call(
        functools.partial(product_kernel, stop_count=stop_count),
        grid=(fine_dev,),
        in_specs=[
            pl.BlockSpec((1, stop_count, block_order, column_count), lambda k: (k, 0, 0, 0)),
        ] + [pl.BlockSpec((1, column_count, vector_count), lambda k: (k, 0, 0))] * stop_count,
        out_specs=pl.BlockSpec((1, block_order, vector_count), lambda k: (k, 0, 0)),
        out_shape=jax.ShapeDtypeStruct((fine_dev, block_order, vector_count), jnp.float32),
        cost_estimate=pl.CostEstimate(
            flops=2 * fine_dev * stop_count * block_order * column_count * vector_count,
            transcendentals=0,
            bytes_accessed=2 * fine_dev * stop_count * block_order * column_count),
    )(hamiltonian, *sources)
    row_block = block_order // band_count
    halves = partial_value.reshape(fine_dev, 2, 2, row_block, vector_count)
    send = lax.dynamic_index_in_dim(halves, 1 - core, 2, keepdims=False)
    keep = lax.dynamic_index_in_dim(halves, core, 2, keepdims=False)
    swap = [(b, b ^ 1) for b in range(band_count)]
    pair_sum = keep + lax.ppermute(send.astype(jnp.bfloat16), "band", swap).astype(jnp.float32)
    level = band // 2
    send = lax.dynamic_index_in_dim(pair_sum, 1 - level, 1, keepdims=False)
    keep = lax.dynamic_index_in_dim(pair_sum, level, 1, keepdims=False)
    swap = [(b, b ^ 2) for b in range(band_count)]
    product_share = (
        keep + lax.ppermute(send.astype(jnp.bfloat16), "band", swap).astype(jnp.float32)
    ).astype(jnp.bfloat16)
    return (hamiltonian, product_share)


def solution(mesh):
    placed = (
        P("blk", None, None),
        P("blk", None, None),
        P("blk", None, None),
        P(),
        P("blk", None, None),
        P("blk", "band", None),
    )
    return jax.shard_map(
        on_device,
        mesh=mesh,
        in_specs=placed,
        out_specs=(P("blk", None, None, "band"), P("blk", "band", None)),
        check_vma=False,
    )
```

```python
import functools

import jax
import jax.numpy as jnp
from jax import lax
from jax.experimental import pallas as pl
from jax.experimental.pallas import tpu as pltpu
from jax.sharding import PartitionSpec as P


def shifted(value, axis, steps):
    count = lax.axis_size(axis)
    pairs = [(source, (source + steps) % count) for source in range(count)]
    return lax.ppermute(value, axis, pairs)


def sandwich_kernel(slot_ref, band_ref, weight_ref, halo_ref, local_ref, inter_ref, right_ref,
                    ham_ref, prod_ref, rot_ref, *, blocks_dev, stop_count, corner_count):
    k = pl.program_id(0)
    column_count = right_ref.shape[2]
    right = right_ref[0]
    sources = [halo_ref.at[slot] for slot in range(blocks_dev)]
    sources += [local_ref.at[slot] for slot in range(blocks_dev)]
    sources += [halo_ref.at[blocks_dev + slot] for slot in range(blocks_dev)]
    for slot, source in enumerate(sources):
        prod_ref[slot] = jnp.dot(source[...], right, preferred_element_type=jnp.float32)
    for s in range(stop_count):
        base = (k * stop_count + s) * corner_count
        rotated = weight_ref[base] * prod_ref[slot_ref[base]]
        for j in range(1, corner_count):
            rotated = rotated + weight_ref[base + j] * prod_ref[slot_ref[base + j]]
        rot_ref[:, s * column_count:(s + 1) * column_count] = rotated.astype(jnp.bfloat16)
    left = inter_ref[0].T
    half = stop_count // 2
    for part in range(2):
        ham = jnp.dot(left, rot_ref[:, part * half * column_count:(part + 1) * half * column_count],
                      preferred_element_type=jnp.float32)
        ham = ham.astype(jnp.bfloat16)
        for s in range(half):
            ham_ref[0, part * half + s] = ham[:, s * column_count:(s + 1) * column_count]


def product_kernel(ham_ref, first_ref, second_ref, third_ref, last_ref, part_ref, *, stop_count):
    wide = jnp.concatenate([ham_ref[0, s] for s in range(stop_count)], axis=1)
    pieces = [first_ref[0]] + [second_ref[j, 0] for j in range(second_ref.shape[0])]
    pieces += [third_ref[j, 0] for j in range(third_ref.shape[0])] + [last_ref[0]]
    tall = jnp.concatenate(pieces, axis=0)
    part_ref[0] = jnp.dot(wide, tall, preferred_element_type=jnp.float32)


def on_device(coarse_kernel, interp_index, interp_weight, stop_order, intersection, trial_vectors):
    blocks_dev = coarse_kernel.shape[0]
    fine_dev = intersection.shape[0]
    column_count = trial_vectors.shape[1]
    vector_count = trial_vectors.shape[2]
    block_order = intersection.shape[1]
    stop_count = stop_order.shape[0]
    corner_count = interp_index.shape[2]
    cycle_length = lax.axis_size("blk")
    total_coarse = blocks_dev * cycle_length
    position = lax.axis_index("blk")
    band = lax.axis_index("band")

    band_count = lax.axis_size("band")
    core = band % 2
    pairs = []
    for i in range(cycle_length):
        for b in range(band_count):
            target = (i + 1) % cycle_length if b % 2 == 0 else (i - 1) % cycle_length
            pairs.append((i * band_count + b, target * band_count + b))
    near = lax.ppermute(coarse_kernel, ("blk", "band"), pairs)
    far = lax.ppermute(near, "band", [(b, b ^ 1) for b in range(band_count)])
    halo = jnp.concatenate([near, far], axis=0)
    assert stop_count == 8
    first = shifted(trial_vectors, "blk", 1)
    last = shifted(trial_vectors, "blk", 8)
    second = shifted(jnp.stack([trial_vectors, first]), "blk", 2)
    third = shifted(jnp.stack([trial_vectors, first, second[0], second[1]]), "blk", 4)
    sources = [first, second, third, last]

    order_index = jnp.take(interp_index, stop_order, axis=1)
    order_weight = jnp.take(interp_weight, stop_order, axis=1)
    window_slots = 3 * blocks_dev
    local_index = jnp.mod(order_index - (position - 1) * blocks_dev, total_coarse)
    slot_group = jnp.clip(local_index // blocks_dev, 0, 2)
    slot_group = jnp.where(core == 0, slot_group, 2 - slot_group)
    slot_index = slot_group * blocks_dev + jnp.mod(local_index, blocks_dev)
    slot_index = jnp.clip(slot_index, 0, window_slots - 1).astype(jnp.int32).reshape(-1)
    weights = order_weight.astype(jnp.float32).reshape(-1)
    band_index = jnp.reshape(band, (1,)).astype(jnp.int32)

    kernel = functools.partial(
        sandwich_kernel, blocks_dev=blocks_dev, stop_count=stop_count, corner_count=corner_count)
    grid_spec = pltpu.PrefetchScalarGridSpec(
        num_scalar_prefetch=2,
        grid=(fine_dev,),
        in_specs=[
            pl.BlockSpec(memory_space=pltpu.SMEM),
            pl.BlockSpec((2 * blocks_dev, block_order, block_order), lambda k, sl, bd: (0, 0, 0)),
            pl.BlockSpec((blocks_dev, block_order, block_order), lambda k, sl, bd: (0, 0, 0)),
            pl.BlockSpec((1, block_order, block_order), lambda k, sl, bd: (k, 0, 0)),
            pl.BlockSpec((1, block_order, column_count), lambda k, sl, bd: (k, 0, bd[0])),
        ],
        out_specs=pl.BlockSpec(
            (1, stop_count, block_order, column_count), lambda k, sl, bd: (k, 0, 0, 0)),
        scratch_shapes=[
            pltpu.VMEM((window_slots, block_order, column_count), jnp.float32),
            pltpu.VMEM((block_order, stop_count * column_count), jnp.bfloat16),
        ],
    )
    hamiltonian = pl.pallas_call(
        kernel,
        grid_spec=grid_spec,
        out_shape=jax.ShapeDtypeStruct(
            (fine_dev, stop_count, block_order, column_count), jnp.bfloat16),
        compiler_params=pltpu.CompilerParams(
            dimension_semantics=("arbitrary",), vmem_limit_bytes=48 * 1024 * 1024),
        cost_estimate=pl.CostEstimate(
            flops=2 * fine_dev * block_order * block_order * column_count * (window_slots + stop_count),
            transcendentals=0,
            bytes_accessed=2 * fine_dev * block_order * (block_order + stop_count * column_count)),
    )(slot_index, band_index, weights, halo, coarse_kernel, intersection, intersection)
    partial_value = pl.pallas_call(
        functools.partial(product_kernel, stop_count=stop_count),
        grid=(fine_dev,),
        in_specs=[
            pl.BlockSpec((1, stop_count, block_order, column_count), lambda k: (k, 0, 0, 0)),
            pl.BlockSpec((1, column_count, vector_count), lambda k: (k, 0, 0)),
            pl.BlockSpec((2, 1, column_count, vector_count), lambda k: (0, k, 0, 0)),
            pl.BlockSpec((4, 1, column_count, vector_count), lambda k: (0, k, 0, 0)),
            pl.BlockSpec((1, column_count, vector_count), lambda k: (k, 0, 0)),
        ],
        out_specs=pl.BlockSpec((1, block_order, vector_count), lambda k: (k, 0, 0)),
        out_shape=jax.ShapeDtypeStruct((fine_dev, block_order, vector_count), jnp.float32),
        cost_estimate=pl.CostEstimate(
            flops=2 * fine_dev * stop_count * block_order * column_count * vector_count,
            transcendentals=0,
            bytes_accessed=2 * fine_dev * stop_count * block_order * column_count),
    )(hamiltonian, *sources)
    row_block = block_order // band_count
    halves = partial_value.reshape(fine_dev, 2, 2, row_block, vector_count)
    send = lax.dynamic_index_in_dim(halves, 1 - core, 2, keepdims=False)
    keep = lax.dynamic_index_in_dim(halves, core, 2, keepdims=False)
    swap = [(b, b ^ 1) for b in range(band_count)]
    pair_sum = keep + lax.ppermute(send.astype(jnp.bfloat16), "band", swap).astype(jnp.float32)
    level = band // 2
    send = lax.dynamic_index_in_dim(pair_sum, 1 - level, 1, keepdims=False)
    keep = lax.dynamic_index_in_dim(pair_sum, level, 1, keepdims=False)
    swap = [(b, b ^ 2) for b in range(band_count)]
    product_share = (
        keep + lax.ppermute(send.astype(jnp.bfloat16), "band", swap).astype(jnp.float32)
    ).astype(jnp.bfloat16)
    return (hamiltonian, product_share)


def solution(mesh):
    placed = (
        P("blk", None, None),
        P("blk", None, None),
        P("blk", None, None),
        P(),
        P("blk", None, None),
        P("blk", "band", None),
    )
    return jax.shard_map(
        on_device,
        mesh=mesh,
        in_specs=placed,
        out_specs=(P("blk", None, None, "band"), P("blk", "band", None)),
        check_vma=False,
    )
```

```python
import functools

import jax
import jax.numpy as jnp
from jax import lax
from jax.experimental import pallas as pl
from jax.experimental.pallas import tpu as pltpu
from jax.sharding import PartitionSpec as P


def shifted(value, axis, steps):
    count = lax.axis_size(axis)
    pairs = [(source, (source + steps) % count) for source in range(count)]
    return lax.ppermute(value, axis, pairs)


def sandwich_kernel(slot_ref, band_ref, weight_ref, halo_ref, local_ref, inter_ref, right_ref,
                    *refs, blocks_dev, stop_count, corner_count, offset):
    ham_ref, prod_ref, rot_ref = refs[-3:]
    k = pl.program_id(0) + offset
    column_count = right_ref.shape[2]
    right = right_ref[0]
    sources = [halo_ref.at[slot] for slot in range(blocks_dev)]
    sources += [local_ref.at[slot] for slot in range(blocks_dev)]
    sources += [halo_ref.at[blocks_dev + slot] for slot in range(blocks_dev)]
    for slot, source in enumerate(sources):
        prod_ref[slot] = jnp.dot(source[...], right, preferred_element_type=jnp.float32)
    for s in range(stop_count):
        base = (k * stop_count + s) * corner_count
        rotated = weight_ref[base] * prod_ref[slot_ref[base]]
        for j in range(1, corner_count):
            rotated = rotated + weight_ref[base + j] * prod_ref[slot_ref[base + j]]
        rot_ref[:, s * column_count:(s + 1) * column_count] = rotated.astype(jnp.bfloat16)
    left = inter_ref[0].T
    half = stop_count // 2
    for part in range(2):
        ham = jnp.dot(left, rot_ref[:, part * half * column_count:(part + 1) * half * column_count],
                      preferred_element_type=jnp.float32)
        ham = ham.astype(jnp.bfloat16)
        for s in range(half):
            ham_ref[0, part * half + s] = ham[:, s * column_count:(s + 1) * column_count]


def product_kernel(ham_ref, odd_ref, even_ref, fourth_ref, last_ref, part_ref, *, stop_count):
    wide = jnp.concatenate([ham_ref[0, s] for s in range(stop_count)], axis=1)
    pieces = [odd_ref[0, 0], even_ref[0, 0], even_ref[1, 0], fourth_ref[0],
              odd_ref[1, 0], even_ref[2, 0], even_ref[3, 0], last_ref[0]]
    tall = jnp.concatenate(pieces, axis=0)
    part_ref[0] = jnp.dot(wide, tall, preferred_element_type=jnp.float32)


def on_device(coarse_kernel, interp_index, interp_weight, stop_order, intersection, trial_vectors):
    blocks_dev = coarse_kernel.shape[0]
    fine_dev = intersection.shape[0]
    column_count = trial_vectors.shape[1]
    vector_count = trial_vectors.shape[2]
    block_order = intersection.shape[1]
    stop_count = stop_order.shape[0]
    corner_count = interp_index.shape[2]
    cycle_length = lax.axis_size("blk")
    total_coarse = blocks_dev * cycle_length
    position = lax.axis_index("blk")
    band = lax.axis_index("band")

    band_count = lax.axis_size("band")
    core = band % 2
    pairs = []
    for i in range(cycle_length):
        for b in range(band_count):
            target = (i + 1) % cycle_length if b % 2 == 0 else (i - 1) % cycle_length
            pairs.append((i * band_count + b, target * band_count + b))
    near = lax.ppermute(coarse_kernel, ("blk", "band"), pairs)
    far = lax.ppermute(near, "band", [(b, b ^ 1) for b in range(band_count)])
    halo = jnp.concatenate([near, far], axis=0)
    assert stop_count == 8
    fourth = shifted(trial_vectors, "blk", 4)
    last = shifted(trial_vectors, "blk", 8)
    odd = shifted(jnp.stack([trial_vectors, fourth]), "blk", 1)


    order_index = jnp.take(interp_index, stop_order, axis=1)
    order_weight = jnp.take(interp_weight, stop_order, axis=1)
    window_slots = 3 * blocks_dev
    local_index = jnp.mod(order_index - (position - 1) * blocks_dev, total_coarse)
    slot_group = jnp.clip(local_index // blocks_dev, 0, 2)
    slot_group = jnp.where(core == 0, slot_group, 2 - slot_group)
    slot_index = slot_group * blocks_dev + jnp.mod(local_index, blocks_dev)
    slot_index = jnp.clip(slot_index, 0, window_slots - 1).astype(jnp.int32).reshape(-1)
    weights = order_weight.astype(jnp.float32).reshape(-1)
    band_index = jnp.reshape(band, (1,)).astype(jnp.int32)

    half_count = fine_dev // 2
    hamiltonian = None
    for offset in (0, half_count):
        kernel = functools.partial(
            sandwich_kernel, blocks_dev=blocks_dev, stop_count=stop_count,
            corner_count=corner_count, offset=offset)
        in_specs = [
            pl.BlockSpec(memory_space=pltpu.SMEM),
            pl.BlockSpec((2 * blocks_dev, block_order, block_order), lambda k, sl, bd: (0, 0, 0)),
            pl.BlockSpec((blocks_dev, block_order, block_order), lambda k, sl, bd: (0, 0, 0)),
            pl.BlockSpec(
                (1, block_order, block_order), lambda k, sl, bd, o=offset: (k + o, 0, 0)),
            pl.BlockSpec(
                (1, block_order, column_count), lambda k, sl, bd, o=offset: (k + o, 0, bd[0])),
        ]
        operands = [slot_index, band_index, weights, halo, coarse_kernel, intersection,
                    intersection]
        aliases = {}
        if hamiltonian is not None:
            in_specs.append(pl.BlockSpec(memory_space=pl.ANY))
            aliases = {len(operands): 0}
            operands.append(hamiltonian)
        grid_spec = pltpu.PrefetchScalarGridSpec(
            num_scalar_prefetch=2,
            grid=(half_count,),
            in_specs=in_specs,
            out_specs=pl.BlockSpec(
                (1, stop_count, block_order, column_count),
                lambda k, sl, bd, o=offset: (k + o, 0, 0, 0)),
            scratch_shapes=[
                pltpu.VMEM((window_slots, block_order, column_count), jnp.float32),
                pltpu.VMEM((block_order, stop_count * column_count), jnp.bfloat16),
            ],
        )
        if hamiltonian is not None:
            hamiltonian, odd = lax.optimization_barrier((hamiltonian, odd))
            even = shifted(jnp.stack([trial_vectors, odd[0], fourth, odd[1]]), "blk", 2)
        hamiltonian = pl.pallas_call(
            kernel,
            grid_spec=grid_spec,
            out_shape=jax.ShapeDtypeStruct(
                (fine_dev, stop_count, block_order, column_count), jnp.bfloat16),
            input_output_aliases=aliases,
            compiler_params=pltpu.CompilerParams(
                dimension_semantics=("arbitrary",), vmem_limit_bytes=48 * 1024 * 1024),
            cost_estimate=pl.CostEstimate(
                flops=half_count * 2 * block_order * block_order * column_count
                * (window_slots + stop_count),
                transcendentals=0,
                bytes_accessed=half_count * 2 * block_order
                * (block_order + stop_count * column_count)),
        )(*operands)
    sources = [odd, even, fourth, last]
    partial_value = pl.pallas_call(
        functools.partial(product_kernel, stop_count=stop_count),
        grid=(fine_dev,),
        in_specs=[
            pl.BlockSpec((1, stop_count, block_order, column_count), lambda k: (k, 0, 0, 0)),
            pl.BlockSpec((2, 1, column_count, vector_count), lambda k: (0, k, 0, 0)),
            pl.BlockSpec((4, 1, column_count, vector_count), lambda k: (0, k, 0, 0)),
            pl.BlockSpec((1, column_count, vector_count), lambda k: (k, 0, 0)),
            pl.BlockSpec((1, column_count, vector_count), lambda k: (k, 0, 0)),
        ],
        out_specs=pl.BlockSpec((1, block_order, vector_count), lambda k: (k, 0, 0)),
        out_shape=jax.ShapeDtypeStruct((fine_dev, block_order, vector_count), jnp.float32),
        cost_estimate=pl.CostEstimate(
            flops=2 * fine_dev * stop_count * block_order * column_count * vector_count,
            transcendentals=0,
            bytes_accessed=2 * fine_dev * stop_count * block_order * column_count),
    )(hamiltonian, *sources)
    row_block = block_order // band_count
    halves = partial_value.reshape(fine_dev, 2, 2, row_block, vector_count)
    send = lax.dynamic_index_in_dim(halves, 1 - core, 2, keepdims=False)
    keep = lax.dynamic_index_in_dim(halves, core, 2, keepdims=False)
    swap = [(b, b ^ 1) for b in range(band_count)]
    pair_sum = keep + lax.ppermute(send.astype(jnp.bfloat16), "band", swap).astype(jnp.float32)
    level = band // 2
    send = lax.dynamic_index_in_dim(pair_sum, 1 - level, 1, keepdims=False)
    keep = lax.dynamic_index_in_dim(pair_sum, level, 1, keepdims=False)
    swap = [(b, b ^ 2) for b in range(band_count)]
    product_share = (
        keep + lax.ppermute(send.astype(jnp.bfloat16), "band", swap).astype(jnp.float32)
    ).astype(jnp.bfloat16)
    return (hamiltonian, product_share)


def solution(mesh):
    placed = (
        P("blk", None, None),
        P("blk", None, None),
        P("blk", None, None),
        P(),
        P("blk", None, None),
        P("blk", "band", None),
    )
    return jax.shard_map(
        on_device,
        mesh=mesh,
        in_specs=placed,
        out_specs=(P("blk", None, None, "band"), P("blk", "band", None)),
        check_vma=False,
    )
```

```python
import functools

import jax
import jax.numpy as jnp
from jax import lax
from jax.experimental import pallas as pl
from jax.experimental.pallas import tpu as pltpu
from jax.sharding import PartitionSpec as P


def shifted(value, axis, steps):
    count = lax.axis_size(axis)
    pairs = [(source, (source + steps) % count) for source in range(count)]
    return lax.ppermute(value, axis, pairs)


def sandwich_kernel(slot_ref, band_ref, weight_ref, halo_ref, local_ref, inter_ref, right_ref,
                    first_ref, second_ref, last_ref, ham_ref, early_ref, prod_ref, rot_ref,
                    *, blocks_dev, stop_count, corner_count):
    k = pl.program_id(0)
    column_count = right_ref.shape[2]
    right = right_ref[0]
    sources = [halo_ref.at[slot] for slot in range(blocks_dev)]
    sources += [local_ref.at[slot] for slot in range(blocks_dev)]
    sources += [halo_ref.at[blocks_dev + slot] for slot in range(blocks_dev)]
    for slot, source in enumerate(sources):
        prod_ref[slot] = jnp.dot(source[...], right, preferred_element_type=jnp.float32)
    for s in range(stop_count):
        base = (k * stop_count + s) * corner_count
        rotated = weight_ref[base] * prod_ref[slot_ref[base]]
        for j in range(1, corner_count):
            rotated = rotated + weight_ref[base + j] * prod_ref[slot_ref[base + j]]
        rot_ref[:, s * column_count:(s + 1) * column_count] = rotated.astype(jnp.bfloat16)
    left = inter_ref[0].T
    half = stop_count // 2
    for part in range(2):
        ham = jnp.dot(left, rot_ref[:, part * half * column_count:(part + 1) * half * column_count],
                      preferred_element_type=jnp.float32)
        ham = ham.astype(jnp.bfloat16)
        for s in range(half):
            ham_ref[0, part * half + s] = ham[:, s * column_count:(s + 1) * column_count]
        if part == 0:
            tall = jnp.concatenate([first_ref[0], second_ref[0, 0], second_ref[1, 0]], axis=0)
            early = jnp.dot(ham[:, :3 * column_count], tall, preferred_element_type=jnp.float32)
        else:
            early = early + jnp.dot(ham[:, (half - 1) * column_count:], last_ref[0],
                                    preferred_element_type=jnp.float32)
    early_ref[0] = early


def product_kernel(ham_ref, early_ref, third_ref, part_ref):
    count = third_ref.shape[0]
    wide = jnp.concatenate([ham_ref[0, 3 + s] for s in range(count)], axis=1)
    tall = jnp.concatenate([third_ref[s, 0] for s in range(count)], axis=0)
    part_ref[0] = early_ref[0] + jnp.dot(wide, tall, preferred_element_type=jnp.float32)


def on_device(coarse_kernel, interp_index, interp_weight, stop_order, intersection, trial_vectors):
    blocks_dev = coarse_kernel.shape[0]
    fine_dev = intersection.shape[0]
    column_count = trial_vectors.shape[1]
    vector_count = trial_vectors.shape[2]
    block_order = intersection.shape[1]
    stop_count = stop_order.shape[0]
    corner_count = interp_index.shape[2]
    cycle_length = lax.axis_size("blk")
    total_coarse = blocks_dev * cycle_length
    position = lax.axis_index("blk")
    band = lax.axis_index("band")

    band_count = lax.axis_size("band")
    core = band % 2
    pairs = []
    for i in range(cycle_length):
        for b in range(band_count):
            target = (i + 1) % cycle_length if b % 2 == 0 else (i - 1) % cycle_length
            pairs.append((i * band_count + b, target * band_count + b))
    near = lax.ppermute(coarse_kernel, ("blk", "band"), pairs)
    far = lax.ppermute(near, "band", [(b, b ^ 1) for b in range(band_count)])
    halo = jnp.concatenate([near, far], axis=0)
    assert stop_count == 8
    first = shifted(trial_vectors, "blk", 1)
    last = shifted(trial_vectors, "blk", 8)
    second = shifted(jnp.stack([trial_vectors, first]), "blk", 2)
    third = shifted(jnp.stack([trial_vectors, first, second[0], second[1]]), "blk", 4)

    order_index = jnp.take(interp_index, stop_order, axis=1)
    order_weight = jnp.take(interp_weight, stop_order, axis=1)
    window_slots = 3 * blocks_dev
    local_index = jnp.mod(order_index - (position - 1) * blocks_dev, total_coarse)
    slot_group = jnp.clip(local_index // blocks_dev, 0, 2)
    slot_group = jnp.where(core == 0, slot_group, 2 - slot_group)
    slot_index = slot_group * blocks_dev + jnp.mod(local_index, blocks_dev)
    slot_index = jnp.clip(slot_index, 0, window_slots - 1).astype(jnp.int32).reshape(-1)
    weights = order_weight.astype(jnp.float32).reshape(-1)
    band_index = jnp.reshape(band, (1,)).astype(jnp.int32)

    kernel = functools.partial(
        sandwich_kernel, blocks_dev=blocks_dev, stop_count=stop_count, corner_count=corner_count)
    grid_spec = pltpu.PrefetchScalarGridSpec(
        num_scalar_prefetch=2,
        grid=(fine_dev,),
        in_specs=[
            pl.BlockSpec(memory_space=pltpu.SMEM),
            pl.BlockSpec((2 * blocks_dev, block_order, block_order), lambda k, sl, bd: (0, 0, 0)),
            pl.BlockSpec((blocks_dev, block_order, block_order), lambda k, sl, bd: (0, 0, 0)),
            pl.BlockSpec((1, block_order, block_order), lambda k, sl, bd: (k, 0, 0)),
            pl.BlockSpec((1, block_order, column_count), lambda k, sl, bd: (k, 0, bd[0])),
            pl.BlockSpec((1, column_count, vector_count), lambda k, sl, bd: (k, 0, 0)),
            pl.BlockSpec((2, 1, column_count, vector_count), lambda k, sl, bd: (0, k, 0, 0)),
            pl.BlockSpec((1, column_count, vector_count), lambda k, sl, bd: (k, 0, 0)),
        ],
        out_specs=[
            pl.BlockSpec(
                (1, stop_count, block_order, column_count), lambda k, sl, bd: (k, 0, 0, 0)),
            pl.BlockSpec((1, block_order, vector_count), lambda k, sl, bd: (k, 0, 0)),
        ],
        scratch_shapes=[
            pltpu.VMEM((window_slots, block_order, column_count), jnp.float32),
            pltpu.VMEM((block_order, stop_count * column_count), jnp.bfloat16),
        ],
    )
    hamiltonian, early_value = pl.pallas_call(
        kernel,
        grid_spec=grid_spec,
        out_shape=[
            jax.ShapeDtypeStruct((fine_dev, stop_count, block_order, column_count), jnp.bfloat16),
            jax.ShapeDtypeStruct((fine_dev, block_order, vector_count), jnp.float32),
        ],
        compiler_params=pltpu.CompilerParams(
            dimension_semantics=("arbitrary",), vmem_limit_bytes=48 * 1024 * 1024),
        cost_estimate=pl.CostEstimate(
            flops=2 * fine_dev * block_order * block_order * column_count * (window_slots + stop_count),
            transcendentals=0,
            bytes_accessed=2 * fine_dev * block_order * (block_order + stop_count * column_count)),
    )(slot_index, band_index, weights, halo, coarse_kernel, intersection, intersection,
      first, second, last)
    partial_value = pl.pallas_call(
        product_kernel,
        grid=(fine_dev,),
        in_specs=[
            pl.BlockSpec((1, stop_count, block_order, column_count), lambda k: (k, 0, 0, 0)),
            pl.BlockSpec((1, block_order, vector_count), lambda k: (k, 0, 0)),
            pl.BlockSpec((4, 1, column_count, vector_count), lambda k: (0, k, 0, 0)),
        ],
        out_specs=pl.BlockSpec((1, block_order, vector_count), lambda k: (k, 0, 0)),
        out_shape=jax.ShapeDtypeStruct((fine_dev, block_order, vector_count), jnp.float32),
        cost_estimate=pl.CostEstimate(
            flops=2 * fine_dev * stop_count * block_order * column_count * vector_count,
            transcendentals=0,
            bytes_accessed=2 * fine_dev * stop_count * block_order * column_count),
    )(hamiltonian, early_value, third)
    row_block = block_order // band_count
    halves = partial_value.reshape(fine_dev, 2, 2, row_block, vector_count)
    send = lax.dynamic_index_in_dim(halves, 1 - core, 2, keepdims=False)
    keep = lax.dynamic_index_in_dim(halves, core, 2, keepdims=False)
    swap = [(b, b ^ 1) for b in range(band_count)]
    pair_sum = keep + lax.ppermute(send.astype(jnp.bfloat16), "band", swap).astype(jnp.float32)
    level = band // 2
    send = lax.dynamic_index_in_dim(pair_sum, 1 - level, 1, keepdims=False)
    keep = lax.dynamic_index_in_dim(pair_sum, level, 1, keepdims=False)
    swap = [(b, b ^ 2) for b in range(band_count)]
    product_share = (
        keep + lax.ppermute(send.astype(jnp.bfloat16), "band", swap).astype(jnp.float32)
    ).astype(jnp.bfloat16)
    return (hamiltonian, product_share)


def solution(mesh):
    placed = (
        P("blk", None, None),
        P("blk", None, None),
        P("blk", None, None),
        P(),
        P("blk", None, None),
        P("blk", "band", None),
    )
    return jax.shard_map(
        on_device,
        mesh=mesh,
        in_specs=placed,
        out_specs=(P("blk", None, None, "band"), P("blk", "band", None)),
        check_vma=False,
    )
```

```python
import functools

import jax
import jax.numpy as jnp
from jax import lax
from jax.experimental import pallas as pl
from jax.experimental.pallas import tpu as pltpu
from jax.sharding import PartitionSpec as P


def shifted(value, axis, steps):
    count = lax.axis_size(axis)
    pairs = [(source, (source + steps) % count) for source in range(count)]
    return lax.ppermute(value, axis, pairs)


def sandwich_kernel(slot_ref, band_ref, weight_ref, halo_ref, local_ref, inter_ref, right_ref,
                    first_ref, second_ref, third_ref, fourth_ref, ham_ref, early_ref, prod_ref,
                    rot_ref,
                    *, blocks_dev, stop_count, corner_count):
    k = pl.program_id(0)
    column_count = right_ref.shape[2]
    right = right_ref[0]
    sources = [halo_ref.at[slot] for slot in range(blocks_dev)]
    sources += [local_ref.at[slot] for slot in range(blocks_dev)]
    sources += [halo_ref.at[blocks_dev + slot] for slot in range(blocks_dev)]
    for slot, source in enumerate(sources):
        prod_ref[slot] = jnp.dot(source[...], right, preferred_element_type=jnp.float32)
    for s in range(stop_count):
        base = (k * stop_count + s) * corner_count
        rotated = weight_ref[base] * prod_ref[slot_ref[base]]
        for j in range(1, corner_count):
            rotated = rotated + weight_ref[base + j] * prod_ref[slot_ref[base + j]]
        rot_ref[:, s * column_count:(s + 1) * column_count] = rotated.astype(jnp.bfloat16)
    left = inter_ref[0].T
    half = stop_count // 2
    for part in range(2):
        ham = jnp.dot(left, rot_ref[:, part * half * column_count:(part + 1) * half * column_count],
                      preferred_element_type=jnp.float32)
        ham = ham.astype(jnp.bfloat16)
        for s in range(half):
            ham_ref[0, part * half + s] = ham[:, s * column_count:(s + 1) * column_count]
        if part == 0:
            tall = jnp.concatenate(
                [first_ref[0], second_ref[0], third_ref[0], fourth_ref[0]], axis=0)
            early_ref[0] = jnp.dot(ham, tall, preferred_element_type=jnp.float32)


def product_kernel(ham_ref, early_ref, late_ref, part_ref):
    count = late_ref.shape[0]
    wide = jnp.concatenate([ham_ref[0, s] for s in range(count)], axis=1)
    tall = jnp.concatenate([late_ref[s, 0] for s in range(count)], axis=0)
    part_ref[0] = early_ref[0] + jnp.dot(wide, tall, preferred_element_type=jnp.float32)


def on_device(coarse_kernel, interp_index, interp_weight, stop_order, intersection, trial_vectors):
    blocks_dev = coarse_kernel.shape[0]
    fine_dev = intersection.shape[0]
    column_count = trial_vectors.shape[1]
    vector_count = trial_vectors.shape[2]
    block_order = intersection.shape[1]
    stop_count = stop_order.shape[0]
    corner_count = interp_index.shape[2]
    cycle_length = lax.axis_size("blk")
    total_coarse = blocks_dev * cycle_length
    position = lax.axis_index("blk")
    band = lax.axis_index("band")

    band_count = lax.axis_size("band")
    core = band % 2
    pairs = []
    for i in range(cycle_length):
        for b in range(band_count):
            target = (i + 1) % cycle_length if b % 2 == 0 else (i - 1) % cycle_length
            pairs.append((i * band_count + b, target * band_count + b))
    near = lax.ppermute(coarse_kernel, ("blk", "band"), pairs)
    far = lax.ppermute(near, "band", [(b, b ^ 1) for b in range(band_count)])
    halo = jnp.concatenate([near, far], axis=0)
    assert stop_count == 8
    first = shifted(trial_vectors, "blk", 1)
    second = shifted(trial_vectors, "blk", 2)
    fourth = shifted(trial_vectors, "blk", 4)
    third = shifted(second, "blk", 1)
    late = shifted(jnp.stack([first, second, third, fourth]), "blk", 4)

    order_index = jnp.take(interp_index, stop_order, axis=1)
    order_weight = jnp.take(interp_weight, stop_order, axis=1)
    window_slots = 3 * blocks_dev
    local_index = jnp.mod(order_index - (position - 1) * blocks_dev, total_coarse)
    slot_group = jnp.clip(local_index // blocks_dev, 0, 2)
    slot_group = jnp.where(core == 0, slot_group, 2 - slot_group)
    slot_index = slot_group * blocks_dev + jnp.mod(local_index, blocks_dev)
    slot_index = jnp.clip(slot_index, 0, window_slots - 1).astype(jnp.int32).reshape(-1)
    weights = order_weight.astype(jnp.float32).reshape(-1)
    band_index = jnp.reshape(band, (1,)).astype(jnp.int32)

    kernel = functools.partial(
        sandwich_kernel, blocks_dev=blocks_dev, stop_count=stop_count, corner_count=corner_count)
    grid_spec = pltpu.PrefetchScalarGridSpec(
        num_scalar_prefetch=2,
        grid=(fine_dev,),
        in_specs=[
            pl.BlockSpec(memory_space=pltpu.SMEM),
            pl.BlockSpec((2 * blocks_dev, block_order, block_order), lambda k, sl, bd: (0, 0, 0)),
            pl.BlockSpec((blocks_dev, block_order, block_order), lambda k, sl, bd: (0, 0, 0)),
            pl.BlockSpec((1, block_order, block_order), lambda k, sl, bd: (k, 0, 0)),
            pl.BlockSpec((1, block_order, column_count), lambda k, sl, bd: (k, 0, bd[0])),
        ] + [pl.BlockSpec((1, column_count, vector_count), lambda k, sl, bd: (k, 0, 0))] * 4,
        out_specs=[
            pl.BlockSpec(
                (1, stop_count, block_order, column_count), lambda k, sl, bd: (k, 0, 0, 0)),
            pl.BlockSpec((1, block_order, vector_count), lambda k, sl, bd: (k, 0, 0)),
        ],
        scratch_shapes=[
            pltpu.VMEM((window_slots, block_order, column_count), jnp.float32),
            pltpu.VMEM((block_order, stop_count * column_count), jnp.bfloat16),
        ],
    )
    hamiltonian, early_value = pl.pallas_call(
        kernel,
        grid_spec=grid_spec,
        out_shape=[
            jax.ShapeDtypeStruct((fine_dev, stop_count, block_order, column_count), jnp.bfloat16),
            jax.ShapeDtypeStruct((fine_dev, block_order, vector_count), jnp.float32),
        ],
        compiler_params=pltpu.CompilerParams(
            dimension_semantics=("arbitrary",), vmem_limit_bytes=48 * 1024 * 1024),
        cost_estimate=pl.CostEstimate(
            flops=2 * fine_dev * block_order * block_order * column_count * (window_slots + stop_count),
            transcendentals=0,
            bytes_accessed=2 * fine_dev * block_order * (block_order + stop_count * column_count)),
    )(slot_index, band_index, weights, halo, coarse_kernel, intersection, intersection,
      first, second, third, fourth)
    partial_value = pl.pallas_call(
        product_kernel,
        grid=(fine_dev,),
        in_specs=[
            pl.BlockSpec((1, stop_count // 2, block_order, column_count), lambda k: (k, 1, 0, 0)),
            pl.BlockSpec((1, block_order, vector_count), lambda k: (k, 0, 0)),
            pl.BlockSpec((stop_count // 2, 1, column_count, vector_count), lambda k: (0, k, 0, 0)),
        ],
        out_specs=pl.BlockSpec((1, block_order, vector_count), lambda k: (k, 0, 0)),
        out_shape=jax.ShapeDtypeStruct((fine_dev, block_order, vector_count), jnp.float32),
        cost_estimate=pl.CostEstimate(
            flops=2 * fine_dev * stop_count * block_order * column_count * vector_count,
            transcendentals=0,
            bytes_accessed=2 * fine_dev * stop_count * block_order * column_count),
    )(hamiltonian, early_value, late)
    row_block = block_order // band_count
    halves = partial_value.reshape(fine_dev, 2, 2, row_block, vector_count)
    send = lax.dynamic_index_in_dim(halves, 1 - core, 2, keepdims=False)
    keep = lax.dynamic_index_in_dim(halves, core, 2, keepdims=False)
    swap = [(b, b ^ 1) for b in range(band_count)]
    pair_sum = keep + lax.ppermute(send.astype(jnp.bfloat16), "band", swap).astype(jnp.float32)
    level = band // 2
    send = lax.dynamic_index_in_dim(pair_sum, 1 - level, 1, keepdims=False)
    keep = lax.dynamic_index_in_dim(pair_sum, level, 1, keepdims=False)
    swap = [(b, b ^ 2) for b in range(band_count)]
    product_share = (
        keep + lax.ppermute(send.astype(jnp.bfloat16), "band", swap).astype(jnp.float32)
    ).astype(jnp.bfloat16)
    return (hamiltonian, product_share)


def solution(mesh):
    placed = (
        P("blk", None, None),
        P("blk", None, None),
        P("blk", None, None),
        P(),
        P("blk", None, None),
        P("blk", "band", None),
    )
    return jax.shard_map(
        on_device,
        mesh=mesh,
        in_specs=placed,
        out_specs=(P("blk", None, None, "band"), P("blk", "band", None)),
        check_vma=False,
    )
```

```python
import functools

import jax
import jax.numpy as jnp
from jax import lax
from jax.experimental import pallas as pl
from jax.experimental.pallas import tpu as pltpu
from jax.sharding import PartitionSpec as P


def shifted(value, axis, steps):
    count = lax.axis_size(axis)
    pairs = [(source, (source + steps) % count) for source in range(count)]
    return lax.ppermute(value, axis, pairs)


def sandwich_kernel(slot_ref, band_ref, weight_ref, halo_ref, local_ref, inter_ref, right_ref,
                    first_ref, second_ref, last_ref, ham_ref, early_ref, prod_ref, rot_ref,
                    *, blocks_dev, stop_count, corner_count):
    k = pl.program_id(0)
    column_count = right_ref.shape[2]
    right = right_ref[0]
    sources = [halo_ref.at[slot] for slot in range(blocks_dev)]
    sources += [local_ref.at[slot] for slot in range(blocks_dev)]
    sources += [halo_ref.at[blocks_dev + slot] for slot in range(blocks_dev)]
    for slot, source in enumerate(sources):
        prod_ref[slot] = jnp.dot(source[...], right, preferred_element_type=jnp.float32)
    for s in range(stop_count):
        base = (k * stop_count + s) * corner_count
        rotated = weight_ref[base] * prod_ref[slot_ref[base]]
        for j in range(1, corner_count):
            rotated = rotated + weight_ref[base + j] * prod_ref[slot_ref[base + j]]
        rot_ref[:, s * column_count:(s + 1) * column_count] = rotated.astype(jnp.bfloat16)
    left = inter_ref[0].T
    half = stop_count // 2
    for part in range(2):
        ham = jnp.dot(left, rot_ref[:, part * half * column_count:(part + 1) * half * column_count],
                      preferred_element_type=jnp.float32)
        ham = ham.astype(jnp.bfloat16)
        for s in range(half):
            ham_ref[0, part * half + s] = ham[:, s * column_count:(s + 1) * column_count]
        if part == 0:
            tall = jnp.concatenate([first_ref[0], second_ref[0, 0], second_ref[1, 0]], axis=0)
            early = jnp.dot(ham[:, :3 * column_count], tall, preferred_element_type=jnp.float32)
        else:
            early = early + jnp.dot(ham[:, (half - 1) * column_count:], last_ref[0],
                                    preferred_element_type=jnp.float32)
    early_ref[0] = early


def product_kernel(ham_ref, early_ref, third_ref, part_ref):
    count = third_ref.shape[0]
    wide = jnp.concatenate([ham_ref[0, 3 + s] for s in range(count)], axis=1)
    tall = jnp.concatenate([third_ref[s, 0] for s in range(count)], axis=0)
    part_ref[0] = early_ref[0] + jnp.dot(wide, tall, preferred_element_type=jnp.float32)


def band_reduce(partial_value, band, band_count):
    fine_count, block_order, vector_count = partial_value.shape
    row_block = block_order // band_count
    core = band % 2
    halves = partial_value.reshape(fine_count, 2, 2, row_block, vector_count)
    send = lax.dynamic_index_in_dim(halves, 1 - core, 2, keepdims=False)
    keep = lax.dynamic_index_in_dim(halves, core, 2, keepdims=False)
    swap = [(b, b ^ 1) for b in range(band_count)]
    pair_sum = keep + lax.ppermute(send.astype(jnp.bfloat16), "band", swap).astype(jnp.float32)
    level = band // 2
    send = lax.dynamic_index_in_dim(pair_sum, 1 - level, 1, keepdims=False)
    keep = lax.dynamic_index_in_dim(pair_sum, level, 1, keepdims=False)
    swap = [(b, b ^ 2) for b in range(band_count)]
    return (
        keep + lax.ppermute(send.astype(jnp.bfloat16), "band", swap).astype(jnp.float32)
    ).astype(jnp.bfloat16)


def on_device(coarse_kernel, interp_index, interp_weight, stop_order, intersection, trial_vectors):
    blocks_dev = coarse_kernel.shape[0]
    fine_dev = intersection.shape[0]
    column_count = trial_vectors.shape[1]
    vector_count = trial_vectors.shape[2]
    block_order = intersection.shape[1]
    stop_count = stop_order.shape[0]
    corner_count = interp_index.shape[2]
    cycle_length = lax.axis_size("blk")
    total_coarse = blocks_dev * cycle_length
    position = lax.axis_index("blk")
    band = lax.axis_index("band")

    band_count = lax.axis_size("band")
    core = band % 2
    pairs = []
    for i in range(cycle_length):
        for b in range(band_count):
            target = (i + 1) % cycle_length if b % 2 == 0 else (i - 1) % cycle_length
            pairs.append((i * band_count + b, target * band_count + b))
    near = lax.ppermute(coarse_kernel, ("blk", "band"), pairs)
    far = lax.ppermute(near, "band", [(b, b ^ 1) for b in range(band_count)])
    halo = jnp.concatenate([near, far], axis=0)
    assert stop_count == 8
    first = shifted(trial_vectors, "blk", 1)
    last = shifted(trial_vectors, "blk", 8)
    second = shifted(jnp.stack([trial_vectors, first]), "blk", 2)
    third = shifted(jnp.stack([trial_vectors, first, second[0], second[1]]), "blk", 4)

    order_index = jnp.take(interp_index, stop_order, axis=1)
    order_weight = jnp.take(interp_weight, stop_order, axis=1)
    window_slots = 3 * blocks_dev
    local_index = jnp.mod(order_index - (position - 1) * blocks_dev, total_coarse)
    slot_group = jnp.clip(local_index // blocks_dev, 0, 2)
    slot_group = jnp.where(core == 0, slot_group, 2 - slot_group)
    slot_index = slot_group * blocks_dev + jnp.mod(local_index, blocks_dev)
    slot_index = jnp.clip(slot_index, 0, window_slots - 1).astype(jnp.int32).reshape(-1)
    weights = order_weight.astype(jnp.float32).reshape(-1)
    band_index = jnp.reshape(band, (1,)).astype(jnp.int32)

    kernel = functools.partial(
        sandwich_kernel, blocks_dev=blocks_dev, stop_count=stop_count, corner_count=corner_count)
    grid_spec = pltpu.PrefetchScalarGridSpec(
        num_scalar_prefetch=2,
        grid=(fine_dev,),
        in_specs=[
            pl.BlockSpec(memory_space=pltpu.SMEM),
            pl.BlockSpec((2 * blocks_dev, block_order, block_order), lambda k, sl, bd: (0, 0, 0)),
            pl.BlockSpec((blocks_dev, block_order, block_order), lambda k, sl, bd: (0, 0, 0)),
            pl.BlockSpec((1, block_order, block_order), lambda k, sl, bd: (k, 0, 0)),
            pl.BlockSpec((1, block_order, column_count), lambda k, sl, bd: (k, 0, bd[0])),
            pl.BlockSpec((1, column_count, vector_count), lambda k, sl, bd: (k, 0, 0)),
            pl.BlockSpec((2, 1, column_count, vector_count), lambda k, sl, bd: (0, k, 0, 0)),
            pl.BlockSpec((1, column_count, vector_count), lambda k, sl, bd: (k, 0, 0)),
        ],
        out_specs=[
            pl.BlockSpec(
                (1, stop_count, block_order, column_count), lambda k, sl, bd: (k, 0, 0, 0)),
            pl.BlockSpec((1, block_order, vector_count), lambda k, sl, bd: (k, 0, 0)),
        ],
        scratch_shapes=[
            pltpu.VMEM((window_slots, block_order, column_count), jnp.float32),
            pltpu.VMEM((block_order, stop_count * column_count), jnp.bfloat16),
        ],
    )
    hamiltonian, early_value = pl.pallas_call(
        kernel,
        grid_spec=grid_spec,
        out_shape=[
            jax.ShapeDtypeStruct((fine_dev, stop_count, block_order, column_count), jnp.bfloat16),
            jax.ShapeDtypeStruct((fine_dev, block_order, vector_count), jnp.float32),
        ],
        compiler_params=pltpu.CompilerParams(
            dimension_semantics=("arbitrary",), vmem_limit_bytes=48 * 1024 * 1024),
        cost_estimate=pl.CostEstimate(
            flops=2 * fine_dev * block_order * block_order * column_count * (window_slots + stop_count),
            transcendentals=0,
            bytes_accessed=2 * fine_dev * block_order * (block_order + stop_count * column_count)),
    )(slot_index, band_index, weights, halo, coarse_kernel, intersection, intersection,
      first, second, last)
    half_count = fine_dev // 2
    shares = []
    for offset in (0, half_count):
        partial_value = pl.pallas_call(
            product_kernel,
            grid=(half_count,),
            in_specs=[
                pl.BlockSpec((1, stop_count, block_order, column_count),
                             lambda k, o=offset: (k + o, 0, 0, 0)),
                pl.BlockSpec((1, block_order, vector_count), lambda k, o=offset: (k + o, 0, 0)),
                pl.BlockSpec((4, 1, column_count, vector_count),
                             lambda k, o=offset: (0, k + o, 0, 0)),
            ],
            out_specs=pl.BlockSpec((1, block_order, vector_count), lambda k: (k, 0, 0)),
            out_shape=jax.ShapeDtypeStruct((half_count, block_order, vector_count), jnp.float32),
            cost_estimate=pl.CostEstimate(
                flops=2 * half_count * 4 * block_order * column_count * vector_count,
                transcendentals=0,
                bytes_accessed=2 * half_count * stop_count * block_order * column_count),
        )(hamiltonian, early_value, third)
        shares.append(band_reduce(partial_value, band, band_count))
    product_share = jnp.concatenate(shares, axis=0)
    return (hamiltonian, product_share)


def solution(mesh):
    placed = (
        P("blk", None, None),
        P("blk", None, None),
        P("blk", None, None),
        P(),
        P("blk", None, None),
        P("blk", "band", None),
    )
    return jax.shard_map(
        on_device,
        mesh=mesh,
        in_specs=placed,
        out_specs=(P("blk", None, None, "band"), P("blk", "band", None)),
        check_vma=False,
    )
```

```python
import functools

import jax
import jax.numpy as jnp
from jax import lax
from jax.experimental import pallas as pl
from jax.experimental.pallas import tpu as pltpu
from jax.sharding import PartitionSpec as P


def shifted(value, axis, steps):
    count = lax.axis_size(axis)
    pairs = [(source, (source + steps) % count) for source in range(count)]
    return lax.ppermute(value, axis, pairs)


def sandwich_kernel(slot_ref, band_ref, weight_ref, halo_ref, local_ref, inter_ref, right_ref,
                    first_ref, second_ref, last_ref, ham_ref, early_ref, prod_ref, rot_ref,
                    *, blocks_dev, stop_count, corner_count):
    k = pl.program_id(0)
    column_count = right_ref.shape[2]
    right = right_ref[0]
    sources = [halo_ref.at[slot] for slot in range(blocks_dev)]
    sources += [local_ref.at[slot] for slot in range(blocks_dev)]
    sources += [halo_ref.at[blocks_dev + slot] for slot in range(blocks_dev)]
    for slot, source in enumerate(sources):
        prod_ref[slot] = jnp.dot(source[...], right, preferred_element_type=jnp.float32)
    for s in range(stop_count):
        base = (k * stop_count + s) * corner_count
        rotated = weight_ref[base] * prod_ref[slot_ref[base]]
        for j in range(1, corner_count):
            rotated = rotated + weight_ref[base + j] * prod_ref[slot_ref[base + j]]
        rot_ref[:, s * column_count:(s + 1) * column_count] = rotated.astype(jnp.bfloat16)
    left = inter_ref[0].T
    half = stop_count // 2
    for part in range(2):
        ham = jnp.dot(left, rot_ref[:, part * half * column_count:(part + 1) * half * column_count],
                      preferred_element_type=jnp.float32)
        ham = ham.astype(jnp.bfloat16)
        for s in range(half):
            ham_ref[0, part * half + s] = ham[:, s * column_count:(s + 1) * column_count]
        if part == 0:
            tall = jnp.concatenate([first_ref[0], second_ref[0, 0], second_ref[1, 0]], axis=0)
            early = jnp.dot(ham[:, :3 * column_count], tall, preferred_element_type=jnp.float32)
        else:
            early = early + jnp.dot(ham[:, (half - 1) * column_count:], last_ref[0],
                                    preferred_element_type=jnp.float32)
    early_ref[0] = early


def product_kernel(ham_ref, early_ref, third_ref, part_ref):
    count = third_ref.shape[0]
    for k in range(ham_ref.shape[0]):
        wide = jnp.concatenate([ham_ref[k, 3 + s] for s in range(count)], axis=1)
        tall = jnp.concatenate([third_ref[s, k] for s in range(count)], axis=0)
        part_ref[k] = early_ref[k] + jnp.dot(wide, tall, preferred_element_type=jnp.float32)


def on_device(coarse_kernel, interp_index, interp_weight, stop_order, intersection, trial_vectors):
    blocks_dev = coarse_kernel.shape[0]
    fine_dev = intersection.shape[0]
    column_count = trial_vectors.shape[1]
    vector_count = trial_vectors.shape[2]
    block_order = intersection.shape[1]
    stop_count = stop_order.shape[0]
    corner_count = interp_index.shape[2]
    cycle_length = lax.axis_size("blk")
    total_coarse = blocks_dev * cycle_length
    position = lax.axis_index("blk")
    band = lax.axis_index("band")

    band_count = lax.axis_size("band")
    core = band % 2
    pairs = []
    for i in range(cycle_length):
        for b in range(band_count):
            target = (i + 1) % cycle_length if b % 2 == 0 else (i - 1) % cycle_length
            pairs.append((i * band_count + b, target * band_count + b))
    near = lax.ppermute(coarse_kernel, ("blk", "band"), pairs)
    far = lax.ppermute(near, "band", [(b, b ^ 1) for b in range(band_count)])
    halo = jnp.concatenate([near, far], axis=0)
    assert stop_count == 8
    first = shifted(trial_vectors, "blk", 1)
    last = shifted(trial_vectors, "blk", 8)
    second = shifted(jnp.stack([trial_vectors, first]), "blk", 2)
    third = shifted(jnp.stack([trial_vectors, first, second[0], second[1]]), "blk", 4)

    order_index = jnp.take(interp_index, stop_order, axis=1)
    order_weight = jnp.take(interp_weight, stop_order, axis=1)
    window_slots = 3 * blocks_dev
    local_index = jnp.mod(order_index - (position - 1) * blocks_dev, total_coarse)
    slot_group = jnp.clip(local_index // blocks_dev, 0, 2)
    slot_group = jnp.where(core == 0, slot_group, 2 - slot_group)
    slot_index = slot_group * blocks_dev + jnp.mod(local_index, blocks_dev)
    slot_index = jnp.clip(slot_index, 0, window_slots - 1).astype(jnp.int32).reshape(-1)
    weights = order_weight.astype(jnp.float32).reshape(-1)
    band_index = jnp.reshape(band, (1,)).astype(jnp.int32)

    kernel = functools.partial(
        sandwich_kernel, blocks_dev=blocks_dev, stop_count=stop_count, corner_count=corner_count)
    grid_spec = pltpu.PrefetchScalarGridSpec(
        num_scalar_prefetch=2,
        grid=(fine_dev,),
        in_specs=[
            pl.BlockSpec(memory_space=pltpu.SMEM),
            pl.BlockSpec((2 * blocks_dev, block_order, block_order), lambda k, sl, bd: (0, 0, 0)),
            pl.BlockSpec((blocks_dev, block_order, block_order), lambda k, sl, bd: (0, 0, 0)),
            pl.BlockSpec((1, block_order, block_order), lambda k, sl, bd: (k, 0, 0)),
            pl.BlockSpec((1, block_order, column_count), lambda k, sl, bd: (k, 0, bd[0])),
            pl.BlockSpec((1, column_count, vector_count), lambda k, sl, bd: (k, 0, 0)),
            pl.BlockSpec((2, 1, column_count, vector_count), lambda k, sl, bd: (0, k, 0, 0)),
            pl.BlockSpec((1, column_count, vector_count), lambda k, sl, bd: (k, 0, 0)),
        ],
        out_specs=[
            pl.BlockSpec(
                (1, stop_count, block_order, column_count), lambda k, sl, bd: (k, 0, 0, 0)),
            pl.BlockSpec((1, block_order, vector_count), lambda k, sl, bd: (k, 0, 0)),
        ],
        scratch_shapes=[
            pltpu.VMEM((window_slots, block_order, column_count), jnp.float32),
            pltpu.VMEM((block_order, stop_count * column_count), jnp.bfloat16),
        ],
    )
    hamiltonian, early_value = pl.pallas_call(
        kernel,
        grid_spec=grid_spec,
        out_shape=[
            jax.ShapeDtypeStruct((fine_dev, stop_count, block_order, column_count), jnp.bfloat16),
            jax.ShapeDtypeStruct((fine_dev, block_order, vector_count), jnp.float32),
        ],
        compiler_params=pltpu.CompilerParams(
            dimension_semantics=("arbitrary",), vmem_limit_bytes=48 * 1024 * 1024),
        cost_estimate=pl.CostEstimate(
            flops=2 * fine_dev * block_order * block_order * column_count * (window_slots + stop_count),
            transcendentals=0,
            bytes_accessed=2 * fine_dev * block_order * (block_order + stop_count * column_count)),
    )(slot_index, band_index, weights, halo, coarse_kernel, intersection, intersection,
      first, second, last)
    partial_value = pl.pallas_call(
        product_kernel,
        grid=(2,),
        in_specs=[
            pl.BlockSpec((fine_dev // 2, stop_count, block_order, column_count),
                         lambda k: (k, 0, 0, 0)),
            pl.BlockSpec((fine_dev // 2, block_order, vector_count), lambda k: (k, 0, 0)),
            pl.BlockSpec((4, fine_dev // 2, column_count, vector_count), lambda k: (0, k, 0, 0)),
        ],
        out_specs=pl.BlockSpec((fine_dev // 2, block_order, vector_count), lambda k: (k, 0, 0)),
        out_shape=jax.ShapeDtypeStruct((fine_dev, block_order, vector_count), jnp.float32),
        cost_estimate=pl.CostEstimate(
            flops=2 * fine_dev * stop_count * block_order * column_count * vector_count,
            transcendentals=0,
            bytes_accessed=2 * fine_dev * stop_count * block_order * column_count),
    )(hamiltonian, early_value, third)
    row_block = block_order // band_count
    halves = partial_value.reshape(fine_dev, 2, 2, row_block, vector_count)
    send = lax.dynamic_index_in_dim(halves, 1 - core, 2, keepdims=False)
    keep = lax.dynamic_index_in_dim(halves, core, 2, keepdims=False)
    swap = [(b, b ^ 1) for b in range(band_count)]
    pair_sum = keep + lax.ppermute(send.astype(jnp.bfloat16), "band", swap).astype(jnp.float32)
    level = band // 2
    send = lax.dynamic_index_in_dim(pair_sum, 1 - level, 1, keepdims=False)
    keep = lax.dynamic_index_in_dim(pair_sum, level, 1, keepdims=False)
    swap = [(b, b ^ 2) for b in range(band_count)]
    product_share = (
        keep + lax.ppermute(send.astype(jnp.bfloat16), "band", swap).astype(jnp.float32)
    ).astype(jnp.bfloat16)
    return (hamiltonian, product_share)


def solution(mesh):
    placed = (
        P("blk", None, None),
        P("blk", None, None),
        P("blk", None, None),
        P(),
        P("blk", None, None),
        P("blk", "band", None),
    )
    return jax.shard_map(
        on_device,
        mesh=mesh,
        in_specs=placed,
        out_specs=(P("blk", None, None, "band"), P("blk", "band", None)),
        check_vma=False,
    )
```

```python
import functools

import jax
import jax.numpy as jnp
from jax import lax
from jax.experimental import pallas as pl
from jax.experimental.pallas import tpu as pltpu
from jax.sharding import PartitionSpec as P


def shifted(value, axis, steps):
    count = lax.axis_size(axis)
    pairs = [(source, (source + steps) % count) for source in range(count)]
    return lax.ppermute(value, axis, pairs)


def sandwich_kernel(slot_ref, band_ref, weight_ref, halo_ref, local_ref, inter_ref, right_ref,
                    first_ref, second_ref, last_ref, ham_ref, early_ref, prod_ref, rot_ref,
                    *, blocks_dev, stop_count, corner_count):
    k = pl.program_id(0)
    column_count = right_ref.shape[2]
    right = right_ref[0]
    sources = [halo_ref.at[slot] for slot in range(blocks_dev)]
    sources += [local_ref.at[slot] for slot in range(blocks_dev)]
    sources += [halo_ref.at[blocks_dev + slot] for slot in range(blocks_dev)]
    for slot, source in enumerate(sources):
        prod_ref[slot] = jnp.dot(source[...], right, preferred_element_type=jnp.float32)
    for s in range(stop_count):
        base = (k * stop_count + s) * corner_count
        rotated = weight_ref[base] * prod_ref[slot_ref[base]]
        for j in range(1, corner_count):
            rotated = rotated + weight_ref[base + j] * prod_ref[slot_ref[base + j]]
        rot_ref[:, s * column_count:(s + 1) * column_count] = rotated.astype(jnp.bfloat16)
    left = inter_ref[0].T
    half = stop_count // 2
    for part in range(2):
        ham = jnp.dot(left, rot_ref[:, part * half * column_count:(part + 1) * half * column_count],
                      preferred_element_type=jnp.float32)
        ham = ham.astype(jnp.bfloat16)
        for s in range(half):
            ham_ref[0, part * half + s] = ham[:, s * column_count:(s + 1) * column_count]
        if part == 0:
            tall = jnp.concatenate([first_ref[0], second_ref[0, 0], second_ref[1, 0]], axis=0)
            early = jnp.dot(ham[:, :3 * column_count], tall, preferred_element_type=jnp.float32)
        else:
            early = early + jnp.dot(ham[:, (half - 1) * column_count:], last_ref[0],
                                    preferred_element_type=jnp.float32)
    early_ref[0] = early


def product_kernel(band_ref, ham_ref, early_ref, third_ref, send_ref, keep_ref, part_ref):
    count = third_ref.shape[0]
    rows = keep_ref.shape[2]
    core = band_ref[0] % 2
    for k in range(ham_ref.shape[0]):
        wide = jnp.concatenate([ham_ref[k, 3 + s] for s in range(count)], axis=1)
        tall = jnp.concatenate([third_ref[s, k] for s in range(count)], axis=0)
        part_ref[...] = early_ref[k] + jnp.dot(wide, tall, preferred_element_type=jnp.float32)
        for level in range(2):
            own = pl.multiple_of((level * 2 + core) * rows, rows)
            other = pl.multiple_of((level * 2 + 1 - core) * rows, rows)
            keep_ref[k, level] = part_ref[pl.ds(own, rows), :]
            send_ref[k, level] = part_ref[pl.ds(other, rows), :].astype(jnp.bfloat16)


def on_device(coarse_kernel, interp_index, interp_weight, stop_order, intersection, trial_vectors):
    blocks_dev = coarse_kernel.shape[0]
    fine_dev = intersection.shape[0]
    column_count = trial_vectors.shape[1]
    vector_count = trial_vectors.shape[2]
    block_order = intersection.shape[1]
    stop_count = stop_order.shape[0]
    corner_count = interp_index.shape[2]
    cycle_length = lax.axis_size("blk")
    total_coarse = blocks_dev * cycle_length
    position = lax.axis_index("blk")
    band = lax.axis_index("band")

    band_count = lax.axis_size("band")
    core = band % 2
    pairs = []
    for i in range(cycle_length):
        for b in range(band_count):
            target = (i + 1) % cycle_length if b % 2 == 0 else (i - 1) % cycle_length
            pairs.append((i * band_count + b, target * band_count + b))
    near = lax.ppermute(coarse_kernel, ("blk", "band"), pairs)
    far = lax.ppermute(near, "band", [(b, b ^ 1) for b in range(band_count)])
    halo = jnp.concatenate([near, far], axis=0)
    assert stop_count == 8
    first = shifted(trial_vectors, "blk", 1)
    last = shifted(trial_vectors, "blk", 8)
    second = shifted(jnp.stack([trial_vectors, first]), "blk", 2)
    third = shifted(jnp.stack([trial_vectors, first, second[0], second[1]]), "blk", 4)

    order_index = jnp.take(interp_index, stop_order, axis=1)
    order_weight = jnp.take(interp_weight, stop_order, axis=1)
    window_slots = 3 * blocks_dev
    local_index = jnp.mod(order_index - (position - 1) * blocks_dev, total_coarse)
    slot_group = jnp.clip(local_index // blocks_dev, 0, 2)
    slot_group = jnp.where(core == 0, slot_group, 2 - slot_group)
    slot_index = slot_group * blocks_dev + jnp.mod(local_index, blocks_dev)
    slot_index = jnp.clip(slot_index, 0, window_slots - 1).astype(jnp.int32).reshape(-1)
    weights = order_weight.astype(jnp.float32).reshape(-1)
    band_index = jnp.reshape(band, (1,)).astype(jnp.int32)

    kernel = functools.partial(
        sandwich_kernel, blocks_dev=blocks_dev, stop_count=stop_count, corner_count=corner_count)
    grid_spec = pltpu.PrefetchScalarGridSpec(
        num_scalar_prefetch=2,
        grid=(fine_dev,),
        in_specs=[
            pl.BlockSpec(memory_space=pltpu.SMEM),
            pl.BlockSpec((2 * blocks_dev, block_order, block_order), lambda k, sl, bd: (0, 0, 0)),
            pl.BlockSpec((blocks_dev, block_order, block_order), lambda k, sl, bd: (0, 0, 0)),
            pl.BlockSpec((1, block_order, block_order), lambda k, sl, bd: (k, 0, 0)),
            pl.BlockSpec((1, block_order, column_count), lambda k, sl, bd: (k, 0, bd[0])),
            pl.BlockSpec((1, column_count, vector_count), lambda k, sl, bd: (k, 0, 0)),
            pl.BlockSpec((2, 1, column_count, vector_count), lambda k, sl, bd: (0, k, 0, 0)),
            pl.BlockSpec((1, column_count, vector_count), lambda k, sl, bd: (k, 0, 0)),
        ],
        out_specs=[
            pl.BlockSpec(
                (1, stop_count, block_order, column_count), lambda k, sl, bd: (k, 0, 0, 0)),
            pl.BlockSpec((1, block_order, vector_count), lambda k, sl, bd: (k, 0, 0)),
        ],
        scratch_shapes=[
            pltpu.VMEM((window_slots, block_order, column_count), jnp.float32),
            pltpu.VMEM((block_order, stop_count * column_count), jnp.bfloat16),
        ],
    )
    hamiltonian, early_value = pl.pallas_call(
        kernel,
        grid_spec=grid_spec,
        out_shape=[
            jax.ShapeDtypeStruct((fine_dev, stop_count, block_order, column_count), jnp.bfloat16),
            jax.ShapeDtypeStruct((fine_dev, block_order, vector_count), jnp.float32),
        ],
        compiler_params=pltpu.CompilerParams(
            dimension_semantics=("arbitrary",), vmem_limit_bytes=48 * 1024 * 1024),
        cost_estimate=pl.CostEstimate(
            flops=2 * fine_dev * block_order * block_order * column_count * (window_slots + stop_count),
            transcendentals=0,
            bytes_accessed=2 * fine_dev * block_order * (block_order + stop_count * column_count)),
    )(slot_index, band_index, weights, halo, coarse_kernel, intersection, intersection,
      first, second, last)
    row_block = block_order // band_count
    half_fine = fine_dev // 2
    send, keep = pl.pallas_call(
        product_kernel,
        grid_spec=pltpu.PrefetchScalarGridSpec(
            num_scalar_prefetch=1,
            grid=(2,),
            in_specs=[
                pl.BlockSpec((half_fine, stop_count, block_order, column_count),
                             lambda k, bd: (k, 0, 0, 0)),
                pl.BlockSpec((half_fine, block_order, vector_count), lambda k, bd: (k, 0, 0)),
                pl.BlockSpec((4, half_fine, column_count, vector_count),
                             lambda k, bd: (0, k, 0, 0)),
            ],
            out_specs=[
                pl.BlockSpec((half_fine, 2, row_block, vector_count), lambda k, bd: (k, 0, 0, 0)),
                pl.BlockSpec((half_fine, 2, row_block, vector_count), lambda k, bd: (k, 0, 0, 0)),
            ],
            scratch_shapes=[pltpu.VMEM((block_order, vector_count), jnp.float32)],
        ),
        out_shape=[
            jax.ShapeDtypeStruct((fine_dev, 2, row_block, vector_count), jnp.bfloat16),
            jax.ShapeDtypeStruct((fine_dev, 2, row_block, vector_count), jnp.float32),
        ],
        cost_estimate=pl.CostEstimate(
            flops=2 * fine_dev * stop_count * block_order * column_count * vector_count,
            transcendentals=0,
            bytes_accessed=2 * fine_dev * stop_count * block_order * column_count),
    )(band_index, hamiltonian, early_value, third)
    swap = [(b, b ^ 1) for b in range(band_count)]
    pair_sum = keep + lax.ppermute(send, "band", swap).astype(jnp.float32)
    level = band // 2
    send = lax.dynamic_index_in_dim(pair_sum, 1 - level, 1, keepdims=False)
    keep = lax.dynamic_index_in_dim(pair_sum, level, 1, keepdims=False)
    swap = [(b, b ^ 2) for b in range(band_count)]
    product_share = (
        keep + lax.ppermute(send.astype(jnp.bfloat16), "band", swap).astype(jnp.float32)
    ).astype(jnp.bfloat16)
    return (hamiltonian, product_share)


def solution(mesh):
    placed = (
        P("blk", None, None),
        P("blk", None, None),
        P("blk", None, None),
        P(),
        P("blk", None, None),
        P("blk", "band", None),
    )
    return jax.shard_map(
        on_device,
        mesh=mesh,
        in_specs=placed,
        out_specs=(P("blk", None, None, "band"), P("blk", "band", None)),
        check_vma=False,
    )
```

```python
import functools

import jax
import jax.numpy as jnp
from jax import lax
from jax.experimental import pallas as pl
from jax.experimental.pallas import tpu as pltpu
from jax.sharding import PartitionSpec as P


def shifted(value, axis, steps):
    count = lax.axis_size(axis)
    pairs = [(source, (source + steps) % count) for source in range(count)]
    return lax.ppermute(value, axis, pairs)


def sandwich_kernel(slot_ref, band_ref, weight_ref, halo_ref, local_ref, inter_ref, right_ref,
                    first_ref, second_ref, last_ref, ham_ref, early_ref, prod_ref, rot_ref,
                    *, blocks_dev, stop_count, corner_count):
    k = pl.program_id(0)
    column_count = right_ref.shape[2]
    right = right_ref[0]
    sources = [halo_ref.at[slot] for slot in range(blocks_dev)]
    sources += [local_ref.at[slot] for slot in range(blocks_dev)]
    sources += [halo_ref.at[blocks_dev + slot] for slot in range(blocks_dev)]
    for slot, source in enumerate(sources):
        prod_ref[slot] = jnp.dot(source[...], right, preferred_element_type=jnp.float32)
    for s in range(stop_count):
        base = (k * stop_count + s) * corner_count
        rotated = weight_ref[base] * prod_ref[slot_ref[base]]
        for j in range(1, corner_count):
            rotated = rotated + weight_ref[base + j] * prod_ref[slot_ref[base + j]]
        rot_ref[:, s * column_count:(s + 1) * column_count] = rotated.astype(jnp.bfloat16)
    left = inter_ref[0].T
    half = stop_count // 2
    for part in range(2):
        ham = jnp.dot(left, rot_ref[:, part * half * column_count:(part + 1) * half * column_count],
                      preferred_element_type=jnp.float32)
        ham = ham.astype(jnp.bfloat16)
        for s in range(half):
            ham_ref[0, part * half + s] = ham[:, s * column_count:(s + 1) * column_count]
        if part == 0:
            tall = jnp.concatenate([first_ref[0], second_ref[0, 0], second_ref[1, 0]], axis=0)
            early = jnp.dot(ham[:, :3 * column_count], tall, preferred_element_type=jnp.float32)
        else:
            early = early + jnp.dot(ham[:, (half - 1) * column_count:], last_ref[0],
                                    preferred_element_type=jnp.float32)
    early_ref[0] = early


def product_kernel(band_ref, ham_ref, early_ref, third_ref, send_ref, keep_ref, part_ref):
    count = third_ref.shape[0]
    rows = keep_ref.shape[2]
    core = band_ref[0] % 2
    for k in range(ham_ref.shape[0]):
        wide = jnp.concatenate([ham_ref[k, 3 + s] for s in range(count)], axis=1)
        tall = jnp.concatenate([third_ref[s, k] for s in range(count)], axis=0)
        part_ref[...] = early_ref[k] + jnp.dot(wide, tall, preferred_element_type=jnp.float32)
        for level in range(2):
            own = pl.multiple_of((level * 2 + core) * rows, rows)
            other = pl.multiple_of((level * 2 + 1 - core) * rows, rows)
            keep_ref[k, level] = part_ref[pl.ds(own, rows), :]
            send_ref[k, level] = part_ref[pl.ds(other, rows), :].astype(jnp.bfloat16)


def on_device(coarse_kernel, interp_index, interp_weight, stop_order, intersection, trial_vectors):
    blocks_dev = coarse_kernel.shape[0]
    fine_dev = intersection.shape[0]
    column_count = trial_vectors.shape[1]
    vector_count = trial_vectors.shape[2]
    block_order = intersection.shape[1]
    stop_count = stop_order.shape[0]
    corner_count = interp_index.shape[2]
    cycle_length = lax.axis_size("blk")
    total_coarse = blocks_dev * cycle_length
    position = lax.axis_index("blk")
    band = lax.axis_index("band")

    band_count = lax.axis_size("band")
    core = band % 2
    pairs = []
    cross = []
    for i in range(cycle_length):
        for b in range(band_count):
            target = (i + 1) % cycle_length if b % 2 == 0 else (i - 1) % cycle_length
            pairs.append((i * band_count + b, target * band_count + (b ^ 2)))
            target = (i + 1) % cycle_length if b % 2 == 1 else (i - 1) % cycle_length
            cross.append((i * band_count + b, target * band_count + (b ^ 3)))
    near = jnp.concatenate([
        lax.ppermute(coarse_kernel[:1], ("blk", "band"), pairs),
        lax.ppermute(coarse_kernel[1:], ("blk", "band"), cross)], axis=0)
    far = lax.ppermute(near, "band", [(b, b ^ 1) for b in range(band_count)])
    halo = jnp.concatenate([near, far], axis=0)
    assert stop_count == 8
    first = shifted(trial_vectors, "blk", 1)
    last = shifted(trial_vectors, "blk", 8)
    second = shifted(jnp.stack([trial_vectors, first]), "blk", 2)
    third = shifted(jnp.stack([trial_vectors, first, second[0], second[1]]), "blk", 4)

    order_index = jnp.take(interp_index, stop_order, axis=1)
    order_weight = jnp.take(interp_weight, stop_order, axis=1)
    window_slots = 3 * blocks_dev
    local_index = jnp.mod(order_index - (position - 1) * blocks_dev, total_coarse)
    slot_group = jnp.clip(local_index // blocks_dev, 0, 2)
    slot_group = jnp.where(core == 0, slot_group, 2 - slot_group)
    slot_index = slot_group * blocks_dev + jnp.mod(local_index, blocks_dev)
    slot_index = jnp.clip(slot_index, 0, window_slots - 1).astype(jnp.int32).reshape(-1)
    weights = order_weight.astype(jnp.float32).reshape(-1)
    band_index = jnp.reshape(band, (1,)).astype(jnp.int32)

    kernel = functools.partial(
        sandwich_kernel, blocks_dev=blocks_dev, stop_count=stop_count, corner_count=corner_count)
    grid_spec = pltpu.PrefetchScalarGridSpec(
        num_scalar_prefetch=2,
        grid=(fine_dev,),
        in_specs=[
            pl.BlockSpec(memory_space=pltpu.SMEM),
            pl.BlockSpec((2 * blocks_dev, block_order, block_order), lambda k, sl, bd: (0, 0, 0)),
            pl.BlockSpec((blocks_dev, block_order, block_order), lambda k, sl, bd: (0, 0, 0)),
            pl.BlockSpec((1, block_order, block_order), lambda k, sl, bd: (k, 0, 0)),
            pl.BlockSpec((1, block_order, column_count), lambda k, sl, bd: (k, 0, bd[0])),
            pl.BlockSpec((1, column_count, vector_count), lambda k, sl, bd: (k, 0, 0)),
            pl.BlockSpec((2, 1, column_count, vector_count), lambda k, sl, bd: (0, k, 0, 0)),
            pl.BlockSpec((1, column_count, vector_count), lambda k, sl, bd: (k, 0, 0)),
        ],
        out_specs=[
            pl.BlockSpec(
                (1, stop_count, block_order, column_count), lambda k, sl, bd: (k, 0, 0, 0)),
            pl.BlockSpec((1, block_order, vector_count), lambda k, sl, bd: (k, 0, 0)),
        ],
        scratch_shapes=[
            pltpu.VMEM((window_slots, block_order, column_count), jnp.float32),
            pltpu.VMEM((block_order, stop_count * column_count), jnp.bfloat16),
        ],
    )
    hamiltonian, early_value = pl.pallas_call(
        kernel,
        grid_spec=grid_spec,
        out_shape=[
            jax.ShapeDtypeStruct((fine_dev, stop_count, block_order, column_count), jnp.bfloat16),
            jax.ShapeDtypeStruct((fine_dev, block_order, vector_count), jnp.float32),
        ],
        compiler_params=pltpu.CompilerParams(
            dimension_semantics=("arbitrary",), vmem_limit_bytes=48 * 1024 * 1024),
        cost_estimate=pl.CostEstimate(
            flops=2 * fine_dev * block_order * block_order * column_count * (window_slots + stop_count),
            transcendentals=0,
            bytes_accessed=2 * fine_dev * block_order * (block_order + stop_count * column_count)),
    )(slot_index, band_index, weights, halo, coarse_kernel, intersection, intersection,
      first, second, last)
    row_block = block_order // band_count
    half_fine = fine_dev // 2
    send, keep = pl.pallas_call(
        product_kernel,
        grid_spec=pltpu.PrefetchScalarGridSpec(
            num_scalar_prefetch=1,
            grid=(2,),
            in_specs=[
                pl.BlockSpec((half_fine, stop_count, block_order, column_count),
                             lambda k, bd: (k, 0, 0, 0)),
                pl.BlockSpec((half_fine, block_order, vector_count), lambda k, bd: (k, 0, 0)),
                pl.BlockSpec((4, half_fine, column_count, vector_count),
                             lambda k, bd: (0, k, 0, 0)),
            ],
            out_specs=[
                pl.BlockSpec((half_fine, 2, row_block, vector_count), lambda k, bd: (k, 0, 0, 0)),
                pl.BlockSpec((half_fine, 2, row_block, vector_count), lambda k, bd: (k, 0, 0, 0)),
            ],
            scratch_shapes=[pltpu.VMEM((block_order, vector_count), jnp.float32)],
        ),
        out_shape=[
            jax.ShapeDtypeStruct((fine_dev, 2, row_block, vector_count), jnp.bfloat16),
            jax.ShapeDtypeStruct((fine_dev, 2, row_block, vector_count), jnp.float32),
        ],
        cost_estimate=pl.CostEstimate(
            flops=2 * fine_dev * stop_count * block_order * column_count * vector_count,
            transcendentals=0,
            bytes_accessed=2 * fine_dev * stop_count * block_order * column_count),
    )(band_index, hamiltonian, early_value, third)
    swap = [(b, b ^ 1) for b in range(band_count)]
    pair_sum = keep + lax.ppermute(send, "band", swap).astype(jnp.float32)
    level = band // 2
    send = lax.dynamic_index_in_dim(pair_sum, 1 - level, 1, keepdims=False)
    keep = lax.dynamic_index_in_dim(pair_sum, level, 1, keepdims=False)
    swap = [(b, b ^ 2) for b in range(band_count)]
    product_share = (
        keep + lax.ppermute(send.astype(jnp.bfloat16), "band", swap).astype(jnp.float32)
    ).astype(jnp.bfloat16)
    return (hamiltonian, product_share)


def solution(mesh):
    placed = (
        P("blk", None, None),
        P("blk", None, None),
        P("blk", None, None),
        P(),
        P("blk", None, None),
        P("blk", "band", None),
    )
    return jax.shard_map(
        on_device,
        mesh=mesh,
        in_specs=placed,
        out_specs=(P("blk", None, None, "band"), P("blk", "band", None)),
        check_vma=False,
    )
```

```python
import functools

import jax
import jax.numpy as jnp
from jax import lax
from jax.experimental import pallas as pl
from jax.experimental.pallas import tpu as pltpu
from jax.sharding import PartitionSpec as P


def shifted(value, axis, steps):
    count = lax.axis_size(axis)
    pairs = [(source, (source + steps) % count) for source in range(count)]
    return lax.ppermute(value, axis, pairs)


def sandwich_kernel(slot_ref, band_ref, weight_ref, halo_ref, local_ref, inter_ref, right_ref,
                    first_ref, second_ref, last_ref, ham_ref, early_ref, prod_ref, rot_ref,
                    *, blocks_dev, stop_count, corner_count):
    k = pl.program_id(0)
    column_count = right_ref.shape[2]
    right = right_ref[0]
    sources = [halo_ref.at[slot] for slot in range(blocks_dev)]
    sources += [local_ref.at[slot] for slot in range(blocks_dev)]
    sources += [halo_ref.at[blocks_dev + slot] for slot in range(blocks_dev)]
    for slot, source in enumerate(sources):
        prod_ref[slot] = jnp.dot(source[...], right, preferred_element_type=jnp.float32)
    for s in range(stop_count):
        base = (k * stop_count + s) * corner_count
        rotated = weight_ref[base] * prod_ref[slot_ref[base]]
        for j in range(1, corner_count):
            rotated = rotated + weight_ref[base + j] * prod_ref[slot_ref[base + j]]
        rot_ref[:, s * column_count:(s + 1) * column_count] = rotated.astype(jnp.bfloat16)
    left = inter_ref[0].T
    half = stop_count // 2
    for part in range(2):
        ham = jnp.dot(left, rot_ref[:, part * half * column_count:(part + 1) * half * column_count],
                      preferred_element_type=jnp.float32)
        ham = ham.astype(jnp.bfloat16)
        for s in range(half):
            ham_ref[0, part * half + s] = ham[:, s * column_count:(s + 1) * column_count]
        if part == 0:
            tall = jnp.concatenate([first_ref[0], second_ref[0, 0], second_ref[1, 0]], axis=0)
            early = jnp.dot(ham[:, :3 * column_count], tall, preferred_element_type=jnp.float32)
        else:
            early = early + jnp.dot(ham[:, (half - 1) * column_count:], last_ref[0],
                                    preferred_element_type=jnp.float32)
    early_ref[0] = early


def product_kernel(band_ref, head_ref, middle_ref, tail_ref, early_ref, third_ref, send_ref,
                   keep_ref, part_ref):
    count = third_ref.shape[0]
    rows = keep_ref.shape[2]
    core = band_ref[0] % 2
    for k in range(head_ref.shape[0]):
        pieces = [head_ref[k, 0], middle_ref[k, 0], middle_ref[k, 1], tail_ref[k, 0]]
        wide = jnp.concatenate(pieces, axis=1)
        tall = jnp.concatenate([third_ref[s, k] for s in range(count)], axis=0)
        part_ref[...] = early_ref[k] + jnp.dot(wide, tall, preferred_element_type=jnp.float32)
        for level in range(2):
            own = pl.multiple_of((level * 2 + core) * rows, rows)
            other = pl.multiple_of((level * 2 + 1 - core) * rows, rows)
            keep_ref[k, level] = part_ref[pl.ds(own, rows), :]
            send_ref[k, level] = part_ref[pl.ds(other, rows), :].astype(jnp.bfloat16)


def on_device(coarse_kernel, interp_index, interp_weight, stop_order, intersection, trial_vectors):
    blocks_dev = coarse_kernel.shape[0]
    fine_dev = intersection.shape[0]
    column_count = trial_vectors.shape[1]
    vector_count = trial_vectors.shape[2]
    block_order = intersection.shape[1]
    stop_count = stop_order.shape[0]
    corner_count = interp_index.shape[2]
    cycle_length = lax.axis_size("blk")
    total_coarse = blocks_dev * cycle_length
    position = lax.axis_index("blk")
    band = lax.axis_index("band")

    band_count = lax.axis_size("band")
    core = band % 2
    pairs = []
    for i in range(cycle_length):
        for b in range(band_count):
            target = (i + 1) % cycle_length if b % 2 == 0 else (i - 1) % cycle_length
            pairs.append((i * band_count + b, target * band_count + b))
    near = lax.ppermute(coarse_kernel, ("blk", "band"), pairs)
    far = lax.ppermute(near, "band", [(b, b ^ 1) for b in range(band_count)])
    halo = jnp.concatenate([near, far], axis=0)
    assert stop_count == 8
    first = shifted(trial_vectors, "blk", 1)
    last = shifted(trial_vectors, "blk", 8)
    second = shifted(jnp.stack([trial_vectors, first]), "blk", 2)
    third = shifted(jnp.stack([trial_vectors, first, second[0], second[1]]), "blk", 4)

    order_index = jnp.take(interp_index, stop_order, axis=1)
    order_weight = jnp.take(interp_weight, stop_order, axis=1)
    window_slots = 3 * blocks_dev
    local_index = jnp.mod(order_index - (position - 1) * blocks_dev, total_coarse)
    slot_group = jnp.clip(local_index // blocks_dev, 0, 2)
    slot_group = jnp.where(core == 0, slot_group, 2 - slot_group)
    slot_index = slot_group * blocks_dev + jnp.mod(local_index, blocks_dev)
    slot_index = jnp.clip(slot_index, 0, window_slots - 1).astype(jnp.int32).reshape(-1)
    weights = order_weight.astype(jnp.float32).reshape(-1)
    band_index = jnp.reshape(band, (1,)).astype(jnp.int32)

    kernel = functools.partial(
        sandwich_kernel, blocks_dev=blocks_dev, stop_count=stop_count, corner_count=corner_count)
    grid_spec = pltpu.PrefetchScalarGridSpec(
        num_scalar_prefetch=2,
        grid=(fine_dev,),
        in_specs=[
            pl.BlockSpec(memory_space=pltpu.SMEM),
            pl.BlockSpec((2 * blocks_dev, block_order, block_order), lambda k, sl, bd: (0, 0, 0)),
            pl.BlockSpec((blocks_dev, block_order, block_order), lambda k, sl, bd: (0, 0, 0)),
            pl.BlockSpec((1, block_order, block_order), lambda k, sl, bd: (k, 0, 0)),
            pl.BlockSpec((1, block_order, column_count), lambda k, sl, bd: (k, 0, bd[0])),
            pl.BlockSpec((1, column_count, vector_count), lambda k, sl, bd: (k, 0, 0)),
            pl.BlockSpec((2, 1, column_count, vector_count), lambda k, sl, bd: (0, k, 0, 0)),
            pl.BlockSpec((1, column_count, vector_count), lambda k, sl, bd: (k, 0, 0)),
        ],
        out_specs=[
            pl.BlockSpec(
                (1, stop_count, block_order, column_count), lambda k, sl, bd: (k, 0, 0, 0)),
            pl.BlockSpec((1, block_order, vector_count), lambda k, sl, bd: (k, 0, 0)),
        ],
        scratch_shapes=[
            pltpu.VMEM((window_slots, block_order, column_count), jnp.float32),
            pltpu.VMEM((block_order, stop_count * column_count), jnp.bfloat16),
        ],
    )
    hamiltonian, early_value = pl.pallas_call(
        kernel,
        grid_spec=grid_spec,
        out_shape=[
            jax.ShapeDtypeStruct((fine_dev, stop_count, block_order, column_count), jnp.bfloat16),
            jax.ShapeDtypeStruct((fine_dev, block_order, vector_count), jnp.float32),
        ],
        compiler_params=pltpu.CompilerParams(
            dimension_semantics=("arbitrary",), vmem_limit_bytes=48 * 1024 * 1024),
        cost_estimate=pl.CostEstimate(
            flops=2 * fine_dev * block_order * block_order * column_count * (window_slots + stop_count),
            transcendentals=0,
            bytes_accessed=2 * fine_dev * block_order * (block_order + stop_count * column_count)),
    )(slot_index, band_index, weights, halo, coarse_kernel, intersection, intersection,
      first, second, last)
    row_block = block_order // band_count
    half_fine = fine_dev // 2
    send, keep = pl.pallas_call(
        product_kernel,
        grid_spec=pltpu.PrefetchScalarGridSpec(
            num_scalar_prefetch=1,
            grid=(2,),
            in_specs=[
                pl.BlockSpec((half_fine, 1, block_order, column_count),
                             lambda k, bd: (k, 3, 0, 0)),
                pl.BlockSpec((half_fine, 2, block_order, column_count),
                             lambda k, bd: (k, 2, 0, 0)),
                pl.BlockSpec((half_fine, 1, block_order, column_count),
                             lambda k, bd: (k, 6, 0, 0)),
                pl.BlockSpec((half_fine, block_order, vector_count), lambda k, bd: (k, 0, 0)),
                pl.BlockSpec((4, half_fine, column_count, vector_count),
                             lambda k, bd: (0, k, 0, 0)),
            ],
            out_specs=[
                pl.BlockSpec((half_fine, 2, row_block, vector_count), lambda k, bd: (k, 0, 0, 0)),
                pl.BlockSpec((half_fine, 2, row_block, vector_count), lambda k, bd: (k, 0, 0, 0)),
            ],
            scratch_shapes=[pltpu.VMEM((block_order, vector_count), jnp.float32)],
        ),
        out_shape=[
            jax.ShapeDtypeStruct((fine_dev, 2, row_block, vector_count), jnp.bfloat16),
            jax.ShapeDtypeStruct((fine_dev, 2, row_block, vector_count), jnp.float32),
        ],
        cost_estimate=pl.CostEstimate(
            flops=2 * fine_dev * stop_count * block_order * column_count * vector_count,
            transcendentals=0,
            bytes_accessed=2 * fine_dev * stop_count * block_order * column_count),
    )(band_index, hamiltonian, hamiltonian, hamiltonian, early_value, third)
    swap = [(b, b ^ 1) for b in range(band_count)]
    pair_sum = keep + lax.ppermute(send, "band", swap).astype(jnp.float32)
    level = band // 2
    send = lax.dynamic_index_in_dim(pair_sum, 1 - level, 1, keepdims=False)
    keep = lax.dynamic_index_in_dim(pair_sum, level, 1, keepdims=False)
    swap = [(b, b ^ 2) for b in range(band_count)]
    product_share = (
        keep + lax.ppermute(send.astype(jnp.bfloat16), "band", swap).astype(jnp.float32)
    ).astype(jnp.bfloat16)
    return (hamiltonian, product_share)


def solution(mesh):
    placed = (
        P("blk", None, None),
        P("blk", None, None),
        P("blk", None, None),
        P(),
        P("blk", None, None),
        P("blk", "band", None),
    )
    return jax.shard_map(
        on_device,
        mesh=mesh,
        in_specs=placed,
        out_specs=(P("blk", None, None, "band"), P("blk", "band", None)),
        check_vma=False,
    )
```

```python
import functools

import jax
import jax.numpy as jnp
from jax import lax
from jax.experimental import pallas as pl
from jax.experimental.pallas import tpu as pltpu
from jax.sharding import PartitionSpec as P


def shifted(value, axis, steps):
    count = lax.axis_size(axis)
    pairs = [(source, (source + steps) % count) for source in range(count)]
    return lax.ppermute(value, axis, pairs)


def sandwich_kernel(slot_ref, band_ref, weight_ref, halo_ref, local_ref, inter_ref, right_ref,
                    first_ref, second_ref, last_ref, ham_ref, early_ref, prod_ref, rot_ref,
                    *, blocks_dev, stop_count, corner_count):
    k = pl.program_id(0)
    column_count = right_ref.shape[2]
    right = right_ref[0]
    sources = [halo_ref.at[slot] for slot in range(blocks_dev)]
    sources += [local_ref.at[slot] for slot in range(blocks_dev)]
    sources += [halo_ref.at[blocks_dev + slot] for slot in range(blocks_dev)]
    for slot, source in enumerate(sources):
        prod_ref[slot] = jnp.dot(source[...], right, preferred_element_type=jnp.float32)
    for s in range(stop_count):
        base = (k * stop_count + s) * corner_count
        rotated = weight_ref[base] * prod_ref[slot_ref[base]]
        for j in range(1, corner_count):
            rotated = rotated + weight_ref[base + j] * prod_ref[slot_ref[base + j]]
        rot_ref[:, s * column_count:(s + 1) * column_count] = rotated.astype(jnp.bfloat16)
    left = inter_ref[0].T
    half = stop_count // 2
    for part in range(2):
        ham = jnp.dot(left, rot_ref[:, part * half * column_count:(part + 1) * half * column_count],
                      preferred_element_type=jnp.float32)
        ham = ham.astype(jnp.bfloat16)
        for s in range(half):
            ham_ref[0, part * half + s] = ham[:, s * column_count:(s + 1) * column_count]
        if part == 0:
            tall = jnp.concatenate([first_ref[0], second_ref[0, 0], second_ref[1, 0]], axis=0)
            early = jnp.dot(ham[:, :3 * column_count], tall, preferred_element_type=jnp.float32)
        else:
            early = early + jnp.dot(ham[:, (half - 1) * column_count:], last_ref[0],
                                    preferred_element_type=jnp.float32)
    early_ref[0] = early


def product_kernel(band_ref, head_ref, middle_ref, tail_ref, early_ref, third_ref, send_ref,
                   keep_ref, part_ref):
    count = third_ref.shape[0]
    rows = keep_ref.shape[2]
    core = band_ref[0] % 2
    for k in range(head_ref.shape[0]):
        pieces = [head_ref[k, 0], middle_ref[k, 0], middle_ref[k, 1], tail_ref[k, 0]]
        wide = jnp.concatenate(pieces, axis=1)
        tall = jnp.concatenate([third_ref[s, k] for s in range(count)], axis=0)
        part_ref[...] = early_ref[k] + jnp.dot(wide, tall, preferred_element_type=jnp.float32)
        for level in range(2):
            own = pl.multiple_of((level * 2 + core) * rows, rows)
            other = pl.multiple_of((level * 2 + 1 - core) * rows, rows)
            keep_ref[k, level] = part_ref[pl.ds(own, rows), :]
            send_ref[k, level] = part_ref[pl.ds(other, rows), :].astype(jnp.bfloat16)


def on_device(coarse_kernel, interp_index, interp_weight, stop_order, intersection, trial_vectors):
    blocks_dev = coarse_kernel.shape[0]
    fine_dev = intersection.shape[0]
    column_count = trial_vectors.shape[1]
    vector_count = trial_vectors.shape[2]
    block_order = intersection.shape[1]
    stop_count = stop_order.shape[0]
    corner_count = interp_index.shape[2]
    cycle_length = lax.axis_size("blk")
    total_coarse = blocks_dev * cycle_length
    position = lax.axis_index("blk")
    band = lax.axis_index("band")

    band_count = lax.axis_size("band")
    core = band % 2
    pairs = []
    for i in range(cycle_length):
        for b in range(band_count):
            target = (i + 1) % cycle_length if b % 2 == 0 else (i - 1) % cycle_length
            pairs.append((i * band_count + b, target * band_count + b))
    near = lax.ppermute(coarse_kernel, ("blk", "band"), pairs)
    far = lax.ppermute(near, "band", [(b, b ^ 1) for b in range(band_count)])
    halo = jnp.concatenate([near, far], axis=0)
    assert stop_count == 8
    first = shifted(trial_vectors, "blk", 1)
    last = shifted(trial_vectors, "blk", 8)
    second = shifted(jnp.stack([trial_vectors, first]), "blk", 2)
    third = shifted(jnp.stack([trial_vectors, first, second[0], second[1]]), "blk", 4)

    order_index = jnp.take(interp_index, stop_order, axis=1)
    order_weight = jnp.take(interp_weight, stop_order, axis=1)
    window_slots = 3 * blocks_dev
    local_index = jnp.mod(order_index - (position - 1) * blocks_dev, total_coarse)
    slot_group = jnp.clip(local_index // blocks_dev, 0, 2)
    slot_group = jnp.where(core == 0, slot_group, 2 - slot_group)
    slot_index = slot_group * blocks_dev + jnp.mod(local_index, blocks_dev)
    slot_index = jnp.clip(slot_index, 0, window_slots - 1).astype(jnp.int32).reshape(-1)
    weights = order_weight.astype(jnp.float32).reshape(-1)
    band_index = jnp.reshape(band, (1,)).astype(jnp.int32)

    kernel = functools.partial(
        sandwich_kernel, blocks_dev=blocks_dev, stop_count=stop_count, corner_count=corner_count)
    grid_spec = pltpu.PrefetchScalarGridSpec(
        num_scalar_prefetch=2,
        grid=(fine_dev,),
        in_specs=[
            pl.BlockSpec(memory_space=pltpu.SMEM),
            pl.BlockSpec((2 * blocks_dev, block_order, block_order), lambda k, sl, bd: (0, 0, 0)),
            pl.BlockSpec((blocks_dev, block_order, block_order), lambda k, sl, bd: (0, 0, 0)),
            pl.BlockSpec((1, block_order, block_order), lambda k, sl, bd: (k, 0, 0)),
            pl.BlockSpec((1, block_order, column_count), lambda k, sl, bd: (k, 0, bd[0])),
            pl.BlockSpec((1, column_count, vector_count), lambda k, sl, bd: (k, 0, 0)),
            pl.BlockSpec((2, 1, column_count, vector_count), lambda k, sl, bd: (0, k, 0, 0)),
            pl.BlockSpec((1, column_count, vector_count), lambda k, sl, bd: (k, 0, 0)),
        ],
        out_specs=[
            pl.BlockSpec(
                (1, stop_count, block_order, column_count), lambda k, sl, bd: (k, 0, 0, 0)),
            pl.BlockSpec((1, block_order, vector_count), lambda k, sl, bd: (k, 0, 0)),
        ],
        scratch_shapes=[
            pltpu.VMEM((window_slots, block_order, column_count), jnp.float32),
            pltpu.VMEM((block_order, stop_count * column_count), jnp.bfloat16),
        ],
    )
    hamiltonian, early_value = pl.pallas_call(
        kernel,
        grid_spec=grid_spec,
        out_shape=[
            jax.ShapeDtypeStruct((fine_dev, stop_count, block_order, column_count), jnp.bfloat16),
            jax.ShapeDtypeStruct((fine_dev, block_order, vector_count), jnp.float32),
        ],
        compiler_params=pltpu.CompilerParams(
            dimension_semantics=("arbitrary",), vmem_limit_bytes=48 * 1024 * 1024),
        cost_estimate=pl.CostEstimate(
            flops=2 * fine_dev * block_order * block_order * column_count * (window_slots + stop_count),
            transcendentals=0,
            bytes_accessed=2 * fine_dev * block_order * (block_order + stop_count * column_count)),
    )(slot_index, band_index, weights, halo, coarse_kernel, intersection, intersection,
      first, second, last)
    row_block = block_order // band_count
    half_fine = fine_dev // 2
    shares = []
    for offset in (0, half_fine):
        send, keep = pl.pallas_call(
            product_kernel,
            grid_spec=pltpu.PrefetchScalarGridSpec(
                num_scalar_prefetch=1,
                grid=(1,),
                in_specs=[
                    pl.BlockSpec((half_fine, 1, block_order, column_count),
                                 lambda k, bd, o=offset // half_fine: (k + o, 3, 0, 0)),
                    pl.BlockSpec((half_fine, 2, block_order, column_count),
                                 lambda k, bd, o=offset // half_fine: (k + o, 2, 0, 0)),
                    pl.BlockSpec((half_fine, 1, block_order, column_count),
                                 lambda k, bd, o=offset // half_fine: (k + o, 6, 0, 0)),
                    pl.BlockSpec((half_fine, block_order, vector_count), lambda k, bd, o=offset // half_fine: (k + o, 0, 0)),
                    pl.BlockSpec((4, half_fine, column_count, vector_count),
                                 lambda k, bd, o=offset // half_fine: (0, k + o, 0, 0)),
                ],
                out_specs=[
                    pl.BlockSpec((half_fine, 2, row_block, vector_count), lambda k, bd: (k, 0, 0, 0)),
                    pl.BlockSpec((half_fine, 2, row_block, vector_count), lambda k, bd: (k, 0, 0, 0)),
                ],
                scratch_shapes=[pltpu.VMEM((block_order, vector_count), jnp.float32)],
            ),
            out_shape=[
                jax.ShapeDtypeStruct((half_fine, 2, row_block, vector_count), jnp.bfloat16),
                jax.ShapeDtypeStruct((half_fine, 2, row_block, vector_count), jnp.float32),
            ],
            cost_estimate=pl.CostEstimate(
                flops=2 * half_fine * stop_count * block_order * column_count * vector_count,
                transcendentals=0,
                bytes_accessed=2 * half_fine * stop_count * block_order * column_count),
        )(band_index, hamiltonian, hamiltonian, hamiltonian, early_value, third)
        swap = [(b, b ^ 1) for b in range(band_count)]
        pair_sum = keep + lax.ppermute(send, "band", swap).astype(jnp.float32)
        level = band // 2
        send = lax.dynamic_index_in_dim(pair_sum, 1 - level, 1, keepdims=False)
        keep = lax.dynamic_index_in_dim(pair_sum, level, 1, keepdims=False)
        swap = [(b, b ^ 2) for b in range(band_count)]
        product_share = (
            keep + lax.ppermute(send.astype(jnp.bfloat16), "band", swap).astype(jnp.float32)
        ).astype(jnp.bfloat16)
        shares.append(product_share)
    product_share = jnp.concatenate(shares, axis=0)
    return (hamiltonian, product_share)


def solution(mesh):
    placed = (
        P("blk", None, None),
        P("blk", None, None),
        P("blk", None, None),
        P(),
        P("blk", None, None),
        P("blk", "band", None),
    )
    return jax.shard_map(
        on_device,
        mesh=mesh,
        in_specs=placed,
        out_specs=(P("blk", None, None, "band"), P("blk", "band", None)),
        check_vma=False,
    )
```

```python
import functools

import jax
import jax.numpy as jnp
from jax import lax
from jax.experimental import pallas as pl
from jax.experimental.pallas import tpu as pltpu
from jax.sharding import PartitionSpec as P


def shifted(value, axis, steps):
    count = lax.axis_size(axis)
    pairs = [(source, (source + steps) % count) for source in range(count)]
    return lax.ppermute(value, axis, pairs)


def sandwich_kernel(slot_ref, band_ref, weight_ref, halo_ref, local_ref, inter_ref, right_ref,
                    first_ref, last_ref, ham_ref, early_ref, prod_ref, rot_ref,
                    *, blocks_dev, stop_count, corner_count):
    k = pl.program_id(0)
    column_count = right_ref.shape[2]
    right = right_ref[0]
    sources = [halo_ref.at[slot] for slot in range(blocks_dev)]
    sources += [local_ref.at[slot] for slot in range(blocks_dev)]
    sources += [halo_ref.at[blocks_dev + slot] for slot in range(blocks_dev)]
    for slot, source in enumerate(sources):
        prod_ref[slot] = jnp.dot(source[...], right, preferred_element_type=jnp.float32)
    for s in range(stop_count):
        base = (k * stop_count + s) * corner_count
        rotated = weight_ref[base] * prod_ref[slot_ref[base]]
        for j in range(1, corner_count):
            rotated = rotated + weight_ref[base + j] * prod_ref[slot_ref[base + j]]
        rot_ref[:, s * column_count:(s + 1) * column_count] = rotated.astype(jnp.bfloat16)
    left = inter_ref[0].T
    half = stop_count // 2
    for part in range(2):
        ham = jnp.dot(left, rot_ref[:, part * half * column_count:(part + 1) * half * column_count],
                      preferred_element_type=jnp.float32)
        ham = ham.astype(jnp.bfloat16)
        for s in range(half):
            ham_ref[0, part * half + s] = ham[:, s * column_count:(s + 1) * column_count]
        if part == 0:
            early = jnp.dot(ham[:, :column_count], first_ref[0], preferred_element_type=jnp.float32)
        else:
            early = early + jnp.dot(ham[:, (half - 1) * column_count:], last_ref[0],
                                    preferred_element_type=jnp.float32)
    early_ref[0] = early


def product_kernel(band_ref, head_ref, low_ref, high_ref, tail_ref, early_ref, two_ref, four_ref,
                   six_ref, send_ref, keep_ref, part_ref):
    rows = keep_ref.shape[2]
    core = band_ref[0] % 2
    for k in range(head_ref.shape[0]):
        pieces = [head_ref[k, 0], low_ref[k, 0], low_ref[k, 1], high_ref[k, 0], high_ref[k, 1],
                  tail_ref[k, 0]]
        wide = jnp.concatenate(pieces, axis=1)
        tall = jnp.concatenate([ref[j, k] for ref in (two_ref, four_ref, six_ref) for j in range(2)],
                               axis=0)
        part_ref[...] = early_ref[k] + jnp.dot(wide, tall, preferred_element_type=jnp.float32)
        for level in range(2):
            own = pl.multiple_of((level * 2 + core) * rows, rows)
            other = pl.multiple_of((level * 2 + 1 - core) * rows, rows)
            keep_ref[k, level] = part_ref[pl.ds(own, rows), :]
            send_ref[k, level] = part_ref[pl.ds(other, rows), :].astype(jnp.bfloat16)


def on_device(coarse_kernel, interp_index, interp_weight, stop_order, intersection, trial_vectors):
    blocks_dev = coarse_kernel.shape[0]
    fine_dev = intersection.shape[0]
    column_count = trial_vectors.shape[1]
    vector_count = trial_vectors.shape[2]
    block_order = intersection.shape[1]
    stop_count = stop_order.shape[0]
    corner_count = interp_index.shape[2]
    cycle_length = lax.axis_size("blk")
    total_coarse = blocks_dev * cycle_length
    position = lax.axis_index("blk")
    band = lax.axis_index("band")

    band_count = lax.axis_size("band")
    core = band % 2
    pairs = []
    for i in range(cycle_length):
        for b in range(band_count):
            target = (i + 1) % cycle_length if b % 2 == 0 else (i - 1) % cycle_length
            pairs.append((i * band_count + b, target * band_count + b))
    near = lax.ppermute(coarse_kernel, ("blk", "band"), pairs)
    far = lax.ppermute(near, "band", [(b, b ^ 1) for b in range(band_count)])
    halo = jnp.concatenate([near, far], axis=0)
    assert stop_count == 8
    first = shifted(trial_vectors, "blk", 1)
    last = shifted(trial_vectors, "blk", 8)
    pair = jnp.stack([trial_vectors, first])
    two = shifted(pair, "blk", 2)
    four = shifted(pair, "blk", 4)
    six = shifted(pair, "blk", 6)

    order_index = jnp.take(interp_index, stop_order, axis=1)
    order_weight = jnp.take(interp_weight, stop_order, axis=1)
    window_slots = 3 * blocks_dev
    local_index = jnp.mod(order_index - (position - 1) * blocks_dev, total_coarse)
    slot_group = jnp.clip(local_index // blocks_dev, 0, 2)
    slot_group = jnp.where(core == 0, slot_group, 2 - slot_group)
    slot_index = slot_group * blocks_dev + jnp.mod(local_index, blocks_dev)
    slot_index = jnp.clip(slot_index, 0, window_slots - 1).astype(jnp.int32).reshape(-1)
    weights = order_weight.astype(jnp.float32).reshape(-1)
    band_index = jnp.reshape(band, (1,)).astype(jnp.int32)

    kernel = functools.partial(
        sandwich_kernel, blocks_dev=blocks_dev, stop_count=stop_count, corner_count=corner_count)
    grid_spec = pltpu.PrefetchScalarGridSpec(
        num_scalar_prefetch=2,
        grid=(fine_dev,),
        in_specs=[
            pl.BlockSpec(memory_space=pltpu.SMEM),
            pl.BlockSpec((2 * blocks_dev, block_order, block_order), lambda k, sl, bd: (0, 0, 0)),
            pl.BlockSpec((blocks_dev, block_order, block_order), lambda k, sl, bd: (0, 0, 0)),
            pl.BlockSpec((1, block_order, block_order), lambda k, sl, bd: (k, 0, 0)),
            pl.BlockSpec((1, block_order, column_count), lambda k, sl, bd: (k, 0, bd[0])),
            pl.BlockSpec((1, column_count, vector_count), lambda k, sl, bd: (k, 0, 0)),
            pl.BlockSpec((1, column_count, vector_count), lambda k, sl, bd: (k, 0, 0)),
        ],
        out_specs=[
            pl.BlockSpec(
                (1, stop_count, block_order, column_count), lambda k, sl, bd: (k, 0, 0, 0)),
            pl.BlockSpec((1, block_order, vector_count), lambda k, sl, bd: (k, 0, 0)),
        ],
        scratch_shapes=[
            pltpu.VMEM((window_slots, block_order, column_count), jnp.float32),
            pltpu.VMEM((block_order, stop_count * column_count), jnp.bfloat16),
        ],
    )
    hamiltonian, early_value = pl.pallas_call(
        kernel,
        grid_spec=grid_spec,
        out_shape=[
            jax.ShapeDtypeStruct((fine_dev, stop_count, block_order, column_count), jnp.bfloat16),
            jax.ShapeDtypeStruct((fine_dev, block_order, vector_count), jnp.float32),
        ],
        compiler_params=pltpu.CompilerParams(
            dimension_semantics=("arbitrary",), vmem_limit_bytes=48 * 1024 * 1024),
        cost_estimate=pl.CostEstimate(
            flops=2 * fine_dev * block_order * block_order * column_count * (window_slots + stop_count),
            transcendentals=0,
            bytes_accessed=2 * fine_dev * block_order * (block_order + stop_count * column_count)),
    )(slot_index, band_index, weights, halo, coarse_kernel, intersection, intersection,
      first, last)
    row_block = block_order // band_count
    half_fine = fine_dev // 2
    send, keep = pl.pallas_call(
        product_kernel,
        grid_spec=pltpu.PrefetchScalarGridSpec(
            num_scalar_prefetch=1,
            grid=(2,),
            in_specs=[
                pl.BlockSpec((half_fine, 1, block_order, column_count),
                             lambda k, bd: (k, 1, 0, 0)),
                pl.BlockSpec((half_fine, 2, block_order, column_count),
                             lambda k, bd: (k, 1, 0, 0)),
                pl.BlockSpec((half_fine, 2, block_order, column_count),
                             lambda k, bd: (k, 2, 0, 0)),
                pl.BlockSpec((half_fine, 1, block_order, column_count),
                             lambda k, bd: (k, 6, 0, 0)),
                pl.BlockSpec((half_fine, block_order, vector_count), lambda k, bd: (k, 0, 0)),
            ] + [pl.BlockSpec((2, half_fine, column_count, vector_count),
                              lambda k, bd: (0, k, 0, 0))] * 3 + [
            ],
            out_specs=[
                pl.BlockSpec((half_fine, 2, row_block, vector_count), lambda k, bd: (k, 0, 0, 0)),
                pl.BlockSpec((half_fine, 2, row_block, vector_count), lambda k, bd: (k, 0, 0, 0)),
            ],
            scratch_shapes=[pltpu.VMEM((block_order, vector_count), jnp.float32)],
        ),
        out_shape=[
            jax.ShapeDtypeStruct((fine_dev, 2, row_block, vector_count), jnp.bfloat16),
            jax.ShapeDtypeStruct((fine_dev, 2, row_block, vector_count), jnp.float32),
        ],
        cost_estimate=pl.CostEstimate(
            flops=2 * fine_dev * stop_count * block_order * column_count * vector_count,
            transcendentals=0,
            bytes_accessed=2 * fine_dev * stop_count * block_order * column_count),
    )(band_index, hamiltonian, hamiltonian, hamiltonian, hamiltonian, early_value, two, four, six)
    swap = [(b, b ^ 1) for b in range(band_count)]
    pair_sum = keep + lax.ppermute(send, "band", swap).astype(jnp.float32)
    level = band // 2
    send = lax.dynamic_index_in_dim(pair_sum, 1 - level, 1, keepdims=False)
    keep = lax.dynamic_index_in_dim(pair_sum, level, 1, keepdims=False)
    swap = [(b, b ^ 2) for b in range(band_count)]
    product_share = (
        keep + lax.ppermute(send.astype(jnp.bfloat16), "band", swap).astype(jnp.float32)
    ).astype(jnp.bfloat16)
    return (hamiltonian, product_share)


def solution(mesh):
    placed = (
        P("blk", None, None),
        P("blk", None, None),
        P("blk", None, None),
        P(),
        P("blk", None, None),
        P("blk", "band", None),
    )
    return jax.shard_map(
        on_device,
        mesh=mesh,
        in_specs=placed,
        out_specs=(P("blk", None, None, "band"), P("blk", "band", None)),
        check_vma=False,
    )
```

```python
import functools

import jax
import jax.numpy as jnp
from jax import lax
from jax.experimental import pallas as pl
from jax.experimental.pallas import tpu as pltpu
from jax.sharding import PartitionSpec as P


def shifted(value, axis, steps):
    count = lax.axis_size(axis)
    pairs = [(source, (source + steps) % count) for source in range(count)]
    return lax.ppermute(value, axis, pairs)


def sandwich_kernel(slot_ref, band_ref, weight_ref, halo_ref, local_ref, inter_ref, right_ref,
                    first_ref, second_ref, last_ref, ham_ref, early_ref, prod_ref, rot_ref,
                    *, blocks_dev, stop_count, corner_count):
    k = pl.program_id(0)
    column_count = right_ref.shape[2]
    right = right_ref[0]
    sources = [halo_ref.at[slot] for slot in range(blocks_dev)]
    sources += [local_ref.at[slot] for slot in range(blocks_dev)]
    sources += [halo_ref.at[blocks_dev + slot] for slot in range(blocks_dev)]
    for slot, source in enumerate(sources):
        prod_ref[slot] = jnp.dot(source[...], right, preferred_element_type=jnp.float32)
    for s in range(stop_count):
        base = (k * stop_count + s) * corner_count
        rotated = weight_ref[base] * prod_ref[slot_ref[base]]
        for j in range(1, corner_count):
            rotated = rotated + weight_ref[base + j] * prod_ref[slot_ref[base + j]]
        rot_ref[:, s * column_count:(s + 1) * column_count] = rotated.astype(jnp.bfloat16)
    left = inter_ref[0].T
    half = stop_count // 2
    for part in range(2):
        ham = jnp.dot(left, rot_ref[:, part * half * column_count:(part + 1) * half * column_count],
                      preferred_element_type=jnp.float32)
        ham = ham.astype(jnp.bfloat16)
        for s in range(half):
            ham_ref[0, part * half + s] = ham[:, s * column_count:(s + 1) * column_count]
        if part == 0:
            tall = jnp.concatenate([first_ref[0], second_ref[0, 0], second_ref[1, 0]], axis=0)
            early = jnp.dot(ham[:, :3 * column_count], tall, preferred_element_type=jnp.float32)
        else:
            early = early + jnp.dot(ham[:, (half - 1) * column_count:], last_ref[0],
                                    preferred_element_type=jnp.float32)
    early_ref[0] = early


def product_kernel(band_ref, head_ref, middle_ref, tail_ref, early_ref, third_ref, send_ref,
                   keep_ref, part_ref):
    count = third_ref.shape[0]
    rows = keep_ref.shape[2]
    core = band_ref[0] % 2
    for k in range(head_ref.shape[0]):
        pieces = [head_ref[k, 0], middle_ref[k, 0], middle_ref[k, 1], tail_ref[k, 0]]
        wide = jnp.concatenate(pieces, axis=1)
        tall = jnp.concatenate([third_ref[s, k] for s in range(count)], axis=0)
        part_ref[...] = early_ref[k] + jnp.dot(wide, tall, preferred_element_type=jnp.float32)
        for level in range(2):
            own = pl.multiple_of((level * 2 + core) * rows, rows)
            other = pl.multiple_of((level * 2 + 1 - core) * rows, rows)
            keep_ref[k, level] = part_ref[pl.ds(own, rows), :]
            send_ref[k, level] = part_ref[pl.ds(other, rows), :].astype(jnp.bfloat16)


def on_device(coarse_kernel, interp_index, interp_weight, stop_order, intersection, trial_vectors):
    blocks_dev = coarse_kernel.shape[0]
    fine_dev = intersection.shape[0]
    column_count = trial_vectors.shape[1]
    vector_count = trial_vectors.shape[2]
    block_order = intersection.shape[1]
    stop_count = stop_order.shape[0]
    corner_count = interp_index.shape[2]
    cycle_length = lax.axis_size("blk")
    total_coarse = blocks_dev * cycle_length
    position = lax.axis_index("blk")
    band = lax.axis_index("band")

    band_count = lax.axis_size("band")
    core = band % 2
    pairs = []
    for i in range(cycle_length):
        for b in range(band_count):
            target = (i + 1) % cycle_length if b % 2 == 0 else (i - 1) % cycle_length
            pairs.append((i * band_count + b, target * band_count + b))
    near = lax.ppermute(coarse_kernel, ("blk", "band"), pairs)
    far = lax.ppermute(near, "band", [(b, b ^ 1) for b in range(band_count)])
    halo = jnp.concatenate([near, far], axis=0)
    assert stop_count == 8
    first = shifted(trial_vectors, "blk", 1)
    last = shifted(trial_vectors, "blk", 8)
    second = shifted(jnp.stack([trial_vectors, first]), "blk", 2)
    third = shifted(jnp.stack([trial_vectors, first, second[0], second[1]]), "blk", 4)

    order_index = jnp.take(interp_index, stop_order, axis=1)
    order_weight = jnp.take(interp_weight, stop_order, axis=1)
    window_slots = 3 * blocks_dev
    local_index = jnp.mod(order_index - (position - 1) * blocks_dev, total_coarse)
    slot_group = jnp.clip(local_index // blocks_dev, 0, 2)
    slot_group = jnp.where(core == 0, slot_group, 2 - slot_group)
    slot_index = slot_group * blocks_dev + jnp.mod(local_index, blocks_dev)
    slot_index = jnp.clip(slot_index, 0, window_slots - 1).astype(jnp.int32).reshape(-1)
    weights = order_weight.astype(jnp.float32).reshape(-1)
    band_index = jnp.reshape(band, (1,)).astype(jnp.int32)

    kernel = functools.partial(
        sandwich_kernel, blocks_dev=blocks_dev, stop_count=stop_count, corner_count=corner_count)
    grid_spec = pltpu.PrefetchScalarGridSpec(
        num_scalar_prefetch=2,
        grid=(fine_dev,),
        in_specs=[
            pl.BlockSpec(memory_space=pltpu.SMEM),
            pl.BlockSpec((2 * blocks_dev, block_order, block_order), lambda k, sl, bd: (0, 0, 0)),
            pl.BlockSpec((blocks_dev, block_order, block_order), lambda k, sl, bd: (0, 0, 0)),
            pl.BlockSpec((1, block_order, block_order), lambda k, sl, bd: (k, 0, 0)),
            pl.BlockSpec((1, block_order, column_count), lambda k, sl, bd: (k, 0, bd[0])),
            pl.BlockSpec((1, column_count, vector_count), lambda k, sl, bd: (k, 0, 0)),
            pl.BlockSpec((2, 1, column_count, vector_count), lambda k, sl, bd: (0, k, 0, 0)),
            pl.BlockSpec((1, column_count, vector_count), lambda k, sl, bd: (k, 0, 0)),
        ],
        out_specs=[
            pl.BlockSpec(
                (1, stop_count, block_order, column_count), lambda k, sl, bd: (k, 0, 0, 0)),
            pl.BlockSpec((1, block_order, vector_count), lambda k, sl, bd: (k, 0, 0)),
        ],
        scratch_shapes=[
            pltpu.VMEM((window_slots, block_order, column_count), jnp.float32),
            pltpu.VMEM((block_order, stop_count * column_count), jnp.bfloat16),
        ],
    )
    hamiltonian, early_value = pl.pallas_call(
        kernel,
        grid_spec=grid_spec,
        out_shape=[
            jax.ShapeDtypeStruct((fine_dev, stop_count, block_order, column_count), jnp.bfloat16),
            jax.ShapeDtypeStruct((fine_dev, block_order, vector_count), jnp.float32),
        ],
        compiler_params=pltpu.CompilerParams(
            dimension_semantics=("arbitrary",), vmem_limit_bytes=48 * 1024 * 1024),
        cost_estimate=pl.CostEstimate(
            flops=2 * fine_dev * block_order * block_order * column_count * (window_slots + stop_count),
            transcendentals=0,
            bytes_accessed=2 * fine_dev * block_order * (block_order + stop_count * column_count)),
    )(slot_index, band_index, weights, halo, coarse_kernel, intersection, intersection,
      first, second, last)
    row_block = block_order // band_count
    half_fine = fine_dev // 4
    send, keep = pl.pallas_call(
        product_kernel,
        grid_spec=pltpu.PrefetchScalarGridSpec(
            num_scalar_prefetch=1,
            grid=(4,),
            in_specs=[
                pl.BlockSpec((half_fine, 1, block_order, column_count),
                             lambda k, bd: (k, 3, 0, 0)),
                pl.BlockSpec((half_fine, 2, block_order, column_count),
                             lambda k, bd: (k, 2, 0, 0)),
                pl.BlockSpec((half_fine, 1, block_order, column_count),
                             lambda k, bd: (k, 6, 0, 0)),
                pl.BlockSpec((half_fine, block_order, vector_count), lambda k, bd: (k, 0, 0)),
                pl.BlockSpec((4, half_fine, column_count, vector_count),
                             lambda k, bd: (0, k, 0, 0)),
            ],
            out_specs=[
                pl.BlockSpec((half_fine, 2, row_block, vector_count), lambda k, bd: (k, 0, 0, 0)),
                pl.BlockSpec((half_fine, 2, row_block, vector_count), lambda k, bd: (k, 0, 0, 0)),
            ],
            scratch_shapes=[pltpu.VMEM((block_order, vector_count), jnp.float32)],
        ),
        out_shape=[
            jax.ShapeDtypeStruct((fine_dev, 2, row_block, vector_count), jnp.bfloat16),
            jax.ShapeDtypeStruct((fine_dev, 2, row_block, vector_count), jnp.float32),
        ],
        cost_estimate=pl.CostEstimate(
            flops=2 * fine_dev * stop_count * block_order * column_count * vector_count,
            transcendentals=0,
            bytes_accessed=2 * fine_dev * stop_count * block_order * column_count),
    )(band_index, hamiltonian, hamiltonian, hamiltonian, early_value, third)
    swap = [(b, b ^ 1) for b in range(band_count)]
    pair_sum = keep + lax.ppermute(send, "band", swap).astype(jnp.float32)
    level = band // 2
    send = lax.dynamic_index_in_dim(pair_sum, 1 - level, 1, keepdims=False)
    keep = lax.dynamic_index_in_dim(pair_sum, level, 1, keepdims=False)
    swap = [(b, b ^ 2) for b in range(band_count)]
    product_share = (
        keep + lax.ppermute(send.astype(jnp.bfloat16), "band", swap).astype(jnp.float32)
    ).astype(jnp.bfloat16)
    return (hamiltonian, product_share)


def solution(mesh):
    placed = (
        P("blk", None, None),
        P("blk", None, None),
        P("blk", None, None),
        P(),
        P("blk", None, None),
        P("blk", "band", None),
    )
    return jax.shard_map(
        on_device,
        mesh=mesh,
        in_specs=placed,
        out_specs=(P("blk", None, None, "band"), P("blk", "band", None)),
        check_vma=False,
    )
```

```python
import functools

import jax
import jax.numpy as jnp
from jax import lax
from jax.experimental import pallas as pl
from jax.experimental.pallas import tpu as pltpu
from jax.sharding import PartitionSpec as P


def shifted(value, axis, steps):
    count = lax.axis_size(axis)
    pairs = [(source, (source + steps) % count) for source in range(count)]
    return lax.ppermute(value, axis, pairs)


def sandwich_kernel(slot_ref, band_ref, weight_ref, halo_ref, local_ref, inter_ref, right_ref,
                    first_ref, second_ref, last_ref, ham_ref, early_ref, prod_ref, rot_ref,
                    *, blocks_dev, stop_count, corner_count):
    k = pl.program_id(0)
    column_count = right_ref.shape[2]
    right = right_ref[0]
    sources = [halo_ref.at[slot] for slot in range(blocks_dev)]
    sources += [local_ref.at[slot] for slot in range(blocks_dev)]
    sources += [halo_ref.at[blocks_dev + slot] for slot in range(blocks_dev)]
    for slot, source in enumerate(sources):
        prod_ref[slot] = jnp.dot(source[...], right, preferred_element_type=jnp.float32)
    for s in range(stop_count):
        base = (k * stop_count + s) * corner_count
        rotated = weight_ref[base] * prod_ref[slot_ref[base]]
        for j in range(1, corner_count):
            rotated = rotated + weight_ref[base + j] * prod_ref[slot_ref[base + j]]
        rot_ref[:, s * column_count:(s + 1) * column_count] = rotated.astype(jnp.bfloat16)
    left = inter_ref[0].T
    half = stop_count // 2
    for part in range(2):
        ham = jnp.dot(left, rot_ref[:, part * half * column_count:(part + 1) * half * column_count],
                      preferred_element_type=jnp.float32)
        ham = ham.astype(jnp.bfloat16)
        for s in range(half):
            ham_ref[0, part * half + s] = ham[:, s * column_count:(s + 1) * column_count]
        if part == 0:
            tall = jnp.concatenate([first_ref[0], second_ref[0, 0], second_ref[1, 0]], axis=0)
            early = jnp.dot(ham[:, :3 * column_count], tall, preferred_element_type=jnp.float32)
        else:
            early = early + jnp.dot(ham[:, (half - 1) * column_count:], last_ref[0],
                                    preferred_element_type=jnp.float32)
    early_ref[0] = early


def product_kernel(band_ref, head_ref, middle_ref, tail_ref, early_ref, third_ref, send_ref,
                   own_ref, other_ref, part_ref):
    count = third_ref.shape[0]
    rows = own_ref.shape[1]
    core = band_ref[0] % 2
    level_own = band_ref[0] // 2
    for k in range(head_ref.shape[0]):
        pieces = [head_ref[k, 0], middle_ref[k, 0], middle_ref[k, 1], tail_ref[k, 0]]
        wide = jnp.concatenate(pieces, axis=1)
        tall = jnp.concatenate([third_ref[s, k] for s in range(count)], axis=0)
        part_ref[...] = early_ref[k] + jnp.dot(wide, tall, preferred_element_type=jnp.float32)
        for level in range(2):
            own = pl.multiple_of((level * 2 + core) * rows, rows)
            other = pl.multiple_of((level * 2 + 1 - core) * rows, rows)
            send_ref[k, level] = part_ref[pl.ds(other, rows), :].astype(jnp.bfloat16)
        own = pl.multiple_of((level_own * 2 + core) * rows, rows)
        other = pl.multiple_of(((1 - level_own) * 2 + core) * rows, rows)
        own_ref[k] = part_ref[pl.ds(own, rows), :]
        other_ref[k] = part_ref[pl.ds(other, rows), :]


def on_device(coarse_kernel, interp_index, interp_weight, stop_order, intersection, trial_vectors):
    blocks_dev = coarse_kernel.shape[0]
    fine_dev = intersection.shape[0]
    column_count = trial_vectors.shape[1]
    vector_count = trial_vectors.shape[2]
    block_order = intersection.shape[1]
    stop_count = stop_order.shape[0]
    corner_count = interp_index.shape[2]
    cycle_length = lax.axis_size("blk")
    total_coarse = blocks_dev * cycle_length
    position = lax.axis_index("blk")
    band = lax.axis_index("band")

    band_count = lax.axis_size("band")
    core = band % 2
    pairs = []
    for i in range(cycle_length):
        for b in range(band_count):
            target = (i + 1) % cycle_length if b % 2 == 0 else (i - 1) % cycle_length
            pairs.append((i * band_count + b, target * band_count + b))
    near = lax.ppermute(coarse_kernel, ("blk", "band"), pairs)
    far = lax.ppermute(near, "band", [(b, b ^ 1) for b in range(band_count)])
    halo = jnp.concatenate([near, far], axis=0)
    assert stop_count == 8
    first = shifted(trial_vectors, "blk", 1)
    last = shifted(trial_vectors, "blk", 8)
    second = shifted(jnp.stack([trial_vectors, first]), "blk", 2)
    third = shifted(jnp.stack([trial_vectors, first, second[0], second[1]]), "blk", 4)

    order_index = jnp.take(interp_index, stop_order, axis=1)
    order_weight = jnp.take(interp_weight, stop_order, axis=1)
    window_slots = 3 * blocks_dev
    local_index = jnp.mod(order_index - (position - 1) * blocks_dev, total_coarse)
    slot_group = jnp.clip(local_index // blocks_dev, 0, 2)
    slot_group = jnp.where(core == 0, slot_group, 2 - slot_group)
    slot_index = slot_group * blocks_dev + jnp.mod(local_index, blocks_dev)
    slot_index = jnp.clip(slot_index, 0, window_slots - 1).astype(jnp.int32).reshape(-1)
    weights = order_weight.astype(jnp.float32).reshape(-1)
    band_index = jnp.reshape(band, (1,)).astype(jnp.int32)

    kernel = functools.partial(
        sandwich_kernel, blocks_dev=blocks_dev, stop_count=stop_count, corner_count=corner_count)
    grid_spec = pltpu.PrefetchScalarGridSpec(
        num_scalar_prefetch=2,
        grid=(fine_dev,),
        in_specs=[
            pl.BlockSpec(memory_space=pltpu.SMEM),
            pl.BlockSpec((2 * blocks_dev, block_order, block_order), lambda k, sl, bd: (0, 0, 0)),
            pl.BlockSpec((blocks_dev, block_order, block_order), lambda k, sl, bd: (0, 0, 0)),
            pl.BlockSpec((1, block_order, block_order), lambda k, sl, bd: (k, 0, 0)),
            pl.BlockSpec((1, block_order, column_count), lambda k, sl, bd: (k, 0, bd[0])),
            pl.BlockSpec((1, column_count, vector_count), lambda k, sl, bd: (k, 0, 0)),
            pl.BlockSpec((2, 1, column_count, vector_count), lambda k, sl, bd: (0, k, 0, 0)),
            pl.BlockSpec((1, column_count, vector_count), lambda k, sl, bd: (k, 0, 0)),
        ],
        out_specs=[
            pl.BlockSpec(
                (1, stop_count, block_order, column_count), lambda k, sl, bd: (k, 0, 0, 0)),
            pl.BlockSpec((1, block_order, vector_count), lambda k, sl, bd: (k, 0, 0)),
        ],
        scratch_shapes=[
            pltpu.VMEM((window_slots, block_order, column_count), jnp.float32),
            pltpu.VMEM((block_order, stop_count * column_count), jnp.bfloat16),
        ],
    )
    hamiltonian, early_value = pl.pallas_call(
        kernel,
        grid_spec=grid_spec,
        out_shape=[
            jax.ShapeDtypeStruct((fine_dev, stop_count, block_order, column_count), jnp.bfloat16),
            jax.ShapeDtypeStruct((fine_dev, block_order, vector_count), jnp.float32),
        ],
        compiler_params=pltpu.CompilerParams(
            dimension_semantics=("arbitrary",), vmem_limit_bytes=48 * 1024 * 1024),
        cost_estimate=pl.CostEstimate(
            flops=2 * fine_dev * block_order * block_order * column_count * (window_slots + stop_count),
            transcendentals=0,
            bytes_accessed=2 * fine_dev * block_order * (block_order + stop_count * column_count)),
    )(slot_index, band_index, weights, halo, coarse_kernel, intersection, intersection,
      first, second, last)
    row_block = block_order // band_count
    half_fine = fine_dev // 2
    send, keep_own, keep_other = pl.pallas_call(
        product_kernel,
        grid_spec=pltpu.PrefetchScalarGridSpec(
            num_scalar_prefetch=1,
            grid=(2,),
            in_specs=[
                pl.BlockSpec((half_fine, 1, block_order, column_count),
                             lambda k, bd: (k, 3, 0, 0)),
                pl.BlockSpec((half_fine, 2, block_order, column_count),
                             lambda k, bd: (k, 2, 0, 0)),
                pl.BlockSpec((half_fine, 1, block_order, column_count),
                             lambda k, bd: (k, 6, 0, 0)),
                pl.BlockSpec((half_fine, block_order, vector_count), lambda k, bd: (k, 0, 0)),
                pl.BlockSpec((4, half_fine, column_count, vector_count),
                             lambda k, bd: (0, k, 0, 0)),
            ],
            out_specs=[
                pl.BlockSpec((half_fine, 2, row_block, vector_count), lambda k, bd: (k, 0, 0, 0)),
                pl.BlockSpec((half_fine, row_block, vector_count), lambda k, bd: (k, 0, 0)),
                pl.BlockSpec((half_fine, row_block, vector_count), lambda k, bd: (k, 0, 0)),
            ],
            scratch_shapes=[pltpu.VMEM((block_order, vector_count), jnp.float32)],
        ),
        out_shape=[
            jax.ShapeDtypeStruct((fine_dev, 2, row_block, vector_count), jnp.bfloat16),
            jax.ShapeDtypeStruct((fine_dev, row_block, vector_count), jnp.float32),
            jax.ShapeDtypeStruct((fine_dev, row_block, vector_count), jnp.float32),
        ],
        cost_estimate=pl.CostEstimate(
            flops=2 * fine_dev * stop_count * block_order * column_count * vector_count,
            transcendentals=0,
            bytes_accessed=2 * fine_dev * stop_count * block_order * column_count),
    )(band_index, hamiltonian, hamiltonian, hamiltonian, early_value, third)
    swap = [(b, b ^ 1) for b in range(band_count)]
    received = lax.ppermute(send, "band", swap).astype(jnp.float32)
    level = band // 2
    send = keep_other + lax.dynamic_index_in_dim(received, 1 - level, 1, keepdims=False)
    keep = keep_own + lax.dynamic_index_in_dim(received, level, 1, keepdims=False)
    swap = [(b, b ^ 2) for b in range(band_count)]
    product_share = (
        keep + lax.ppermute(send.astype(jnp.bfloat16), "band", swap).astype(jnp.float32)
    ).astype(jnp.bfloat16)
    return (hamiltonian, product_share)


def solution(mesh):
    placed = (
        P("blk", None, None),
        P("blk", None, None),
        P("blk", None, None),
        P(),
        P("blk", None, None),
        P("blk", "band", None),
    )
    return jax.shard_map(
        on_device,
        mesh=mesh,
        in_specs=placed,
        out_specs=(P("blk", None, None, "band"), P("blk", "band", None)),
        check_vma=False,
    )
```
